1024 devices in a mesh: gx: 16 (over x, y_hi, core), gy: 64 (over y_lo, z).
Axes of the slice: x: 4, y: 8 (y_hi: 2, y_lo: 4; y = y_hi * 4 + y_lo), z: 16, core: 2. Of those that a mesh axis runs over, the one named last changes fastest.
Arguments:
- potential: float32 [256, 1024, 256], P('gx', 'gy'), may hold values from -1 to 1
- charge: float32 [256, 1024, 256], P('gx', 'gy'), may hold values from -6 to 6
- region: int32 [256, 1024, 256], P('gx', 'gy'), may hold values from 0 to 16, as said below
- electrode_volts: float32 [16], replicated, may hold values from -2 to 2
Outputs:
- correction: float32 [256, 1024, 256], P('gx', 'gy')
The draws below stay inside these ranges and needn't reach their ends.
Inputs may be any that keep to these rules, and one draw needn't show every extreme that they name: `region`: 0 marks a free cell; k marks a cell of electrode k, held at electrode_volts[k - 1]; about one cell in eight belongs to an electrode.
All inputs are finite; a program needn't handle non-finite values.
Results may differ from the reference program's by a relative error of at most 0.00002.
Values sent between devices are 32-bit elements; how exact they have to be, the bound alone decides.
No kernel may reach another device: no remote copies, remote signals or barrier semaphores. Data moves between devices by JAX's collectives and lax.ppermute only.
A program may use at most 64 MiB of HBM per device.

```python
import jax
import jax.numpy as jnp

CZ = 256
LEVELS = 4
SWEEPS = 1
COARSE_SWEEPS = 4
REGIONS = 16
NX = 256
NY = 1024


def draw_region(key, part):
    first_key, second_key = jax.random.split(key)
    picked = jax.random.randint(first_key, (NX, NY, CZ), 0, 8)
    electrode_ids = jax.random.randint(second_key, (NX, NY, CZ), 1, REGIONS + 1)
    return jnp.where(picked == 0, electrode_ids, 0).astype(jnp.int32)


def block_levels(own_key, dims, shards, low, largest):
    loudness, own = 1.0, jax.random.fold_in(own_key, 6)
    for axis_at, parts in shards:
        heights = jnp.exp(jax.random.uniform(jax.random.fold_in(own, axis_at), (parts,), jnp.float32, low / len(shards), largest / len(shards)))
        loudness = loudness * jnp.repeat(heights, dims[axis_at] // parts).reshape([-1 if axis == axis_at else 1 for axis in range(len(dims))])
    return loudness


def normal_values(stream_key, shape, deviation, reach, cuts=(), kind=jnp.bfloat16):
    entries = jax.random.normal(stream_key, shape, jnp.float32) * deviation
    if len(cuts) > 0:
        entries = block_levels(stream_key, shape, cuts, -0.22, 0.18) * entries
    return jnp.clip(entries, min=-reach, max=reach).astype(kind)


def setup_inputs(seed: int = 0) -> dict:
    keys = jax.random.split(jax.random.key(seed), 5)
    return {
        "potential": jnp.clip(jax.random.uniform(keys[0], (NX, NY, CZ), jnp.float32, -1.0, 1.0) * block_levels(keys[0], (NX, NY, CZ), ((0, 16), (1, 64)), -0.4, 0.0), -1.0, 1.0),
        "charge": normal_values(keys[1], (NX, NY, CZ), 1.0, 6.0, ((0, 16), (1, 64)), jnp.float32),
        "region": draw_region(jax.random.fold_in(keys[4], 71), 0),
        "electrode_volts": jnp.clip(jax.random.uniform(keys[3], (REGIONS,), jnp.float32, -2.0, 2.0), -2.0, 2.0),
    }


screen = 0.5


def pad_plane(values):
    return jnp.pad(values, ((1, 1), (1, 1), (0, 0)))


def neighbour_sums(padded):
    interior = padded[1:-1, 1:-1]
    flat_sum = padded[2:, 1:-1] + padded[:-2, 1:-1] + padded[1:-1, 2:] + padded[1:-1, :-2]
    padded_z = jnp.pad(interior, ((0, 0), (0, 0), (1, 1)))
    vertical = padded_z[:, :, 2:] + padded_z[:, :, :-2]
    return flat_sum, vertical


def checker(span_x, span_y, span_z):
    index_x = jnp.arange(span_x, dtype=jnp.int32)[:, None, None]
    index_y = jnp.arange(span_y, dtype=jnp.int32)[None, :, None]
    index_z = jnp.arange(span_z, dtype=jnp.int32)[None, None, :]
    return (index_x + index_y + index_z) % 2


def half_sweep(iterate, source, divisor, weight, movable, colour):
    flat_sum, vertical = neighbour_sums(pad_plane(iterate))
    renewed = (source + weight * flat_sum + vertical) / divisor
    span_x, span_y, span_z = iterate.shape
    update = checker(span_x, span_y, span_z) == colour
    if movable is not None:
        update = jnp.logical_and(update, movable)
    return jnp.where(update, renewed, iterate)


def full_sweep(iterate, source, divisor, weight, movable):
    iterate = half_sweep(iterate, source, divisor, weight, movable, 0)
    return half_sweep(iterate, source, divisor, weight, movable, 1)


def restrict(values):
    paired = values.reshape(values.shape[0] // 2, 2, values.shape[1], values.shape[2])
    even_rows, odd_rows = paired[:, 0], paired[:, 1]
    before = jnp.concatenate([jnp.zeros_like(odd_rows[:1]), odd_rows[:-1]], axis=0)
    across = 0.25 * before + 0.5 * even_rows + 0.25 * odd_rows
    paired = across.reshape(across.shape[0], across.shape[1] // 2, 2, across.shape[2])
    even_rows, odd_rows = paired[:, :, 0], paired[:, :, 1]
    before = jnp.concatenate([jnp.zeros_like(odd_rows[:, :1]), odd_rows[:, :-1]], axis=1)
    return 0.25 * before + 0.5 * even_rows + 0.25 * odd_rows


def coarsen(values):
    paired = values.reshape(values.shape[0] // 2, 2, values.shape[1], values.shape[2])
    across = 0.5 * (paired[:, 0] + paired[:, 1])
    paired = across.reshape(across.shape[0], across.shape[1] // 2, 2, across.shape[2])
    return 0.5 * (paired[:, :, 0] + paired[:, :, 1])


def solve_level(grid_level, source, coefficient, iterate, movable):
    weight = 0.25 ** grid_level
    divisor = (4.0 * weight + 2.0) + coefficient
    if grid_level == LEVELS - 1:
        for sweep_index in range(COARSE_SWEEPS):
            iterate = full_sweep(iterate, source, divisor, weight, None)
        return iterate
    for sweep_index in range(SWEEPS):
        iterate = full_sweep(iterate, source, divisor, weight, movable)
    flat_sum, vertical = neighbour_sums(pad_plane(iterate))
    residual = source - (divisor * iterate - (weight * flat_sum + vertical))
    if movable is not None:
        residual = jnp.where(movable, residual, 0.0)
    coarse_source = restrict(residual)
    coarse_coefficient = coarsen(coefficient)
    coarse = solve_level(grid_level + 1, coarse_source, coarse_coefficient, jnp.zeros_like(coarse_source), None)
    lifted = jnp.repeat(jnp.repeat(coarse, 2, axis=0), 2, axis=1)
    if movable is not None:
        lifted = jnp.where(movable, lifted, 0.0)
    iterate = iterate + lifted
    for sweep_index in range(SWEEPS):
        iterate = full_sweep(iterate, source, divisor, weight, movable)
    return iterate


def reference(potential, charge, region, electrode_volts):
    movable = region == 0
    dirichlet = jnp.zeros_like(potential)
    for electrode in range(REGIONS):
        dirichlet = dirichlet + jnp.where(region == electrode + 1, electrode_volts[electrode], jnp.float32(0.0))
    flat_sum, vertical = neighbour_sums(pad_plane(potential))
    source = charge - (6.0 * potential - (flat_sum + vertical)) - screen * (jnp.exp(potential) - 1.0)
    coefficient = screen * jnp.exp(potential)
    return solve_level(0, source, coefficient, dirichlet, movable)
```

```python
import jax
import jax.numpy as jnp
from jax import lax
from jax.sharding import PartitionSpec as P

screen = 0.5

HALO_FINE = 4
HALO_MID = 4
HALO_COARSE = 2


def shifted(block, axis, distance):
    count = lax.axis_size(axis)
    route = [(i, i + distance) for i in range(count) if 0 <= i + distance < count]
    return lax.ppermute(block, axis, route)


def exchange(block, width):
    block = jnp.concatenate(
        [shifted(block[-width:], "gx", 1), block, shifted(block[:width], "gx", -1)], axis=0
    )
    return jnp.concatenate(
        [shifted(block[:, -width:], "gy", 1), block, shifted(block[:, :width], "gy", -1)], axis=1
    )


def exchange_many(arrays, width):
    depth = arrays[0].shape[2]
    packed = exchange(jnp.concatenate(arrays, axis=2), width)
    return [packed[:, :, i * depth:(i + 1) * depth] for i in range(len(arrays))]


def inside(span_x, span_y, width):
    index_x = lax.axis_index("gx") * span_x - width + jnp.arange(span_x + 2 * width)
    index_y = lax.axis_index("gy") * span_y - width + jnp.arange(span_y + 2 * width)
    total_x = span_x * lax.axis_size("gx")
    total_y = span_y * lax.axis_size("gy")
    keep_x = (index_x >= 0) & (index_x < total_x)
    keep_y = (index_y >= 0) & (index_y < total_y)
    return (keep_x[:, None] & keep_y[None, :])[:, :, None]


def pad_plane(values):
    return jnp.pad(values, ((1, 1), (1, 1), (0, 0)))


def neighbour_sums(padded):
    interior = padded[1:-1, 1:-1]
    flat_sum = padded[2:, 1:-1] + padded[:-2, 1:-1] + padded[1:-1, 2:] + padded[1:-1, :-2]
    padded_z = jnp.pad(interior, ((0, 0), (0, 0), (1, 1)))
    vertical = padded_z[:, :, 2:] + padded_z[:, :, :-2]
    return (flat_sum, vertical)


def checker(span_x, span_y, span_z):
    index_x = jnp.arange(span_x, dtype=jnp.int32)[:, None, None]
    index_y = jnp.arange(span_y, dtype=jnp.int32)[None, :, None]
    index_z = jnp.arange(span_z, dtype=jnp.int32)[None, None, :]
    return (index_x + index_y + index_z) % 2


def half_sweep(iterate, source, divisor, weight, allowed, colour):
    flat_sum, vertical = neighbour_sums(pad_plane(iterate))
    renewed = (source + weight * flat_sum + vertical) / divisor
    span_x, span_y, span_z = iterate.shape
    update = jnp.logical_and(checker(span_x, span_y, span_z) == colour, allowed)
    return jnp.where(update, renewed, iterate)


def sweeps(iterate, source, divisor, weight, allowed, count):
    for _ in range(count):
        iterate = half_sweep(iterate, source, divisor, weight, allowed, 0)
        iterate = half_sweep(iterate, source, divisor, weight, allowed, 1)
    return iterate


def residual_of(iterate, source, divisor, weight, allowed):
    flat_sum, vertical = neighbour_sums(pad_plane(iterate))
    residual = source - (divisor * iterate - (weight * flat_sum + vertical))
    return jnp.where(allowed, residual, 0.0)


def restrict(values, width, span_x, span_y):
    rows = values[width - 1:width + span_x]
    before = rows[:-1].reshape(span_x // 2, 2, *rows.shape[1:])[:, 0]
    paired = rows[1:].reshape(span_x // 2, 2, *rows.shape[1:])
    across = 0.25 * before + 0.5 * paired[:, 0] + 0.25 * paired[:, 1]
    cols = across[:, width - 1:width + span_y]
    before = cols[:, :-1].reshape(cols.shape[0], span_y // 2, 2, cols.shape[2])[:, :, 0]
    paired = cols[:, 1:].reshape(cols.shape[0], span_y // 2, 2, cols.shape[2])
    return 0.25 * before + 0.5 * paired[:, :, 0] + 0.25 * paired[:, :, 1]


def coarsen(values):
    paired = values.reshape(values.shape[0] // 2, 2, values.shape[1], values.shape[2])
    across = 0.5 * (paired[:, 0] + paired[:, 1])
    paired = across.reshape(across.shape[0], across.shape[1] // 2, 2, across.shape[2])
    return 0.5 * (paired[:, :, 0] + paired[:, :, 1])


def lift(coarse):
    return jnp.repeat(jnp.repeat(coarse, 2, axis=0), 2, axis=1)


def interior(values, width):
    return values[width:values.shape[0] - width, width:values.shape[1] - width]


def descend(grid_level, source, coefficient, width):
    span_x, span_y = source.shape[0], source.shape[1]
    source, coefficient_ext = exchange_many([source, coefficient], width)
    weight = 0.25**grid_level
    divisor = 4.0 * weight + 2.0 + coefficient_ext
    allowed = inside(span_x, span_y, width)
    iterate = sweeps(jnp.zeros_like(source), source, divisor, weight, allowed, 1)
    residual = residual_of(iterate, source, divisor, weight, allowed)
    coarse_source = restrict(residual, width, span_x, span_y)
    coarse_coefficient = coarsen(interior(coefficient_ext, width))
    return iterate, source, divisor, weight, allowed, coarse_source, coarse_coefficient


def coarsest(source, coefficient, width):
    span_x, span_y = source.shape[0], source.shape[1]
    source, coefficient = exchange_many([source, coefficient], width)
    weight = 0.25**3
    divisor = 4.0 * weight + 2.0 + coefficient
    allowed = inside(span_x, span_y, width)
    iterate = jnp.zeros_like(source)
    plan = [(0, 1, 0), (1, 0), (1, 0), (1,)]
    for step, colours in enumerate(plan):
        if step > 0:
            iterate = exchange(interior(iterate, width), width)
        for colour in colours:
            iterate = half_sweep(iterate, source, divisor, weight, allowed, colour)
    return iterate


def body(potential, charge, region, electrode_volts):
    span_x, span_y = potential.shape[0], potential.shape[1]
    dirichlet = jnp.zeros_like(potential)
    for electrode in range(electrode_volts.shape[0]):
        dirichlet = dirichlet + jnp.where(
            region == electrode + 1, electrode_volts[electrode], jnp.float32(0.0)
        )
    width = HALO_FINE
    potential, charge, region_f, dirichlet = exchange_many(
        [potential, charge, region.astype(jnp.float32), dirichlet], width
    )
    movable = jnp.logical_and(region_f == 0.0, inside(span_x, span_y, width))
    flat_sum, vertical = neighbour_sums(pad_plane(potential))
    source = (
        charge - (6.0 * potential - (flat_sum + vertical)) - screen * (jnp.exp(potential) - 1.0)
    )
    coefficient = screen * jnp.exp(potential)
    divisor = 4.0 * 1.0 + 2.0 + coefficient
    iterate = sweeps(dirichlet, source, divisor, 1.0, movable, 1)
    residual = residual_of(iterate, source, divisor, 1.0, movable)
    source_1 = restrict(residual, width, span_x, span_y)
    coefficient_1 = coarsen(interior(coefficient, width))

    level_1 = descend(1, source_1, coefficient_1, HALO_MID)
    level_2 = descend(2, level_1[5], level_1[6], HALO_MID)
    iterate_3 = coarsest(level_2[5], level_2[6], HALO_COARSE)

    iterate_2, source_2, divisor_2, weight_2, allowed_2 = level_2[:5]
    iterate_2 = sweeps(iterate_2 + lift(iterate_3), source_2, divisor_2, weight_2, allowed_2, 1)
    iterate_2 = exchange(interior(iterate_2, HALO_MID), HALO_MID // 2)

    iterate_1, source_1, divisor_1, weight_1, allowed_1 = level_1[:5]
    iterate_1 = sweeps(iterate_1 + lift(iterate_2), source_1, divisor_1, weight_1, allowed_1, 1)
    lifted = lift(interior(iterate_1, HALO_MID // 2))

    iterate = iterate + jnp.where(movable, lifted, 0.0)
    iterate = sweeps(iterate, source, divisor, 1.0, movable, 1)
    return interior(iterate, width)


def solution(mesh):
    placed = (P("gx", "gy", None), P("gx", "gy", None), P("gx", "gy", None), P())
    return jax.shard_map(
        body, mesh=mesh, in_specs=placed, out_specs=P("gx", "gy", None), check_vma=False
    )
```

```python
import jax
import jax.numpy as jnp
from jax import lax
from jax.experimental import pallas as pl
from jax.experimental.pallas import tpu as pltpu
from jax.sharding import PartitionSpec as P

screen = 0.5

HALO_FINE = 4
HALO_MID = 4
HALO_COARSE = 2


def shifted(block, axis, distance):
    count = lax.axis_size(axis)
    route = [(i, i + distance) for i in range(count) if 0 <= i + distance < count]
    return lax.ppermute(block, axis, route)


def exchange(block, width):
    block = jnp.concatenate(
        [shifted(block[-width:], "gx", 1), block, shifted(block[:width], "gx", -1)], axis=0
    )
    return jnp.concatenate(
        [shifted(block[:, -width:], "gy", 1), block, shifted(block[:, :width], "gy", -1)], axis=1
    )


def exchange_y(block, width):
    return jnp.concatenate(
        [shifted(block[:, -width:], "gy", 1), block, shifted(block[:, :width], "gy", -1)], axis=1
    )


def gather_x(block):
    count, index = lax.axis_size("gx"), lax.axis_index("gx")
    step = 1
    while step < count:
        other = lax.ppermute(block, "gx", [(i, i ^ step) for i in range(count)])
        lower = (index & step) == 0
        block = jnp.where(
            lower, jnp.concatenate([block, other], axis=0), jnp.concatenate([other, block], axis=0)
        )
        step *= 2
    return block


def exchange_many(arrays, width, exchanger=exchange):
    depth = arrays[0].shape[2]
    packed = exchanger(jnp.concatenate(arrays, axis=2), width)
    return [packed[:, :, i * depth:(i + 1) * depth] for i in range(len(arrays))]


def inside(span_x, span_y, width, whole_x=False):
    index_y = lax.axis_index("gy") * span_y - width + jnp.arange(span_y + 2 * width)
    total_y = span_y * lax.axis_size("gy")
    keep_y = (index_y >= 0) & (index_y < total_y)
    if whole_x:
        return jnp.broadcast_to(keep_y[None, :, None], (span_x, span_y + 2 * width, 1))
    index_x = lax.axis_index("gx") * span_x - width + jnp.arange(span_x + 2 * width)
    total_x = span_x * lax.axis_size("gx")
    keep_x = (index_x >= 0) & (index_x < total_x)
    return (keep_x[:, None] & keep_y[None, :])[:, :, None]


def pad_plane(values):
    return jnp.pad(values, ((1, 1), (1, 1), (0, 0)))


def neighbour_sums(padded):
    interior = padded[1:-1, 1:-1]
    flat_sum = padded[2:, 1:-1] + padded[:-2, 1:-1] + padded[1:-1, 2:] + padded[1:-1, :-2]
    padded_z = jnp.pad(interior, ((0, 0), (0, 0), (1, 1)))
    vertical = padded_z[:, :, 2:] + padded_z[:, :, :-2]
    return (flat_sum, vertical)


def checker(span_x, span_y, span_z):
    index_x = jnp.arange(span_x, dtype=jnp.int32)[:, None, None]
    index_y = jnp.arange(span_y, dtype=jnp.int32)[None, :, None]
    index_z = jnp.arange(span_z, dtype=jnp.int32)[None, None, :]
    return (index_x + index_y + index_z) % 2


def half_sweep(iterate, source, divisor, weight, allowed, colour):
    flat_sum, vertical = neighbour_sums(pad_plane(iterate))
    renewed = (source + weight * flat_sum + vertical) / divisor
    span_x, span_y, span_z = iterate.shape
    update = jnp.logical_and(checker(span_x, span_y, span_z) == colour, allowed)
    return jnp.where(update, renewed, iterate)


def sweeps(iterate, source, divisor, weight, allowed, count):
    for _ in range(count):
        iterate = half_sweep(iterate, source, divisor, weight, allowed, 0)
        iterate = half_sweep(iterate, source, divisor, weight, allowed, 1)
    return iterate


def residual_of(iterate, source, divisor, weight, allowed):
    flat_sum, vertical = neighbour_sums(pad_plane(iterate))
    residual = source - (divisor * iterate - (weight * flat_sum + vertical))
    return jnp.where(allowed, residual, 0.0)


def restrict(values, width_x, width_y, span_x, span_y):
    rows = values[width_x - 1:width_x + span_x]
    before = rows[:-1].reshape(span_x // 2, 2, *rows.shape[1:])[:, 0]
    paired = rows[1:].reshape(span_x // 2, 2, *rows.shape[1:])
    across = 0.25 * before + 0.5 * paired[:, 0] + 0.25 * paired[:, 1]
    cols = across[:, width_y - 1:width_y + span_y]
    before = cols[:, :-1].reshape(cols.shape[0], span_y // 2, 2, cols.shape[2])[:, :, 0]
    paired = cols[:, 1:].reshape(cols.shape[0], span_y // 2, 2, cols.shape[2])
    return 0.25 * before + 0.5 * paired[:, :, 0] + 0.25 * paired[:, :, 1]


def coarsen(values):
    paired = values.reshape(values.shape[0] // 2, 2, values.shape[1], values.shape[2])
    across = 0.5 * (paired[:, 0] + paired[:, 1])
    paired = across.reshape(across.shape[0], across.shape[1] // 2, 2, across.shape[2])
    return 0.5 * (paired[:, :, 0] + paired[:, :, 1])


def lift(coarse):
    return jnp.repeat(jnp.repeat(coarse, 2, axis=0), 2, axis=1)


def interior(values, width):
    return values[width:values.shape[0] - width, width:values.shape[1] - width]


def descend(grid_level, source, coefficient, width):
    span_x, span_y = source.shape[0], source.shape[1]
    source, coefficient_ext = exchange_many([source, coefficient], width)
    weight = 0.25**grid_level
    divisor = 4.0 * weight + 2.0 + coefficient_ext
    allowed = inside(span_x, span_y, width)
    iterate = sweeps(jnp.zeros_like(source), source, divisor, weight, allowed, 1)
    residual = residual_of(iterate, source, divisor, weight, allowed)
    coarse_source = restrict(residual, width, width, span_x, span_y)
    coarse_coefficient = coarsen(interior(coefficient_ext, width))
    return iterate, source, divisor, weight, allowed, coarse_source, coarse_coefficient


def descend_whole_x(grid_level, source, coefficient, width):
    span_y = source.shape[1]
    source, coefficient = exchange_many([source, coefficient], width, exchange_y)
    span_x = source.shape[0]
    weight = 0.25**grid_level
    divisor = 4.0 * weight + 2.0 + coefficient
    allowed = inside(span_x, span_y, width, whole_x=True)
    iterate = sweeps(jnp.zeros_like(source), source, divisor, weight, allowed, 1)
    residual = residual_of(iterate, source, divisor, weight, allowed)
    residual = jnp.pad(residual, ((1, 0), (0, 0), (0, 0)))
    coarse_source = restrict(residual, 1, width, span_x, span_y)
    coarse_coefficient = coarsen(coefficient[:, width:width + span_y])
    return iterate, source, divisor, weight, allowed, coarse_source, coarse_coefficient


def coarsest_whole_x(source, coefficient, width):
    span_y = source.shape[1]
    source, coefficient = exchange_many([source, coefficient], width, exchange_y)
    span_x = source.shape[0]
    weight = 0.25**3
    divisor = 4.0 * weight + 2.0 + coefficient
    allowed = inside(span_x, span_y, width, whole_x=True)
    iterate = jnp.zeros_like(source)
    plan = [(0, 1, 0), (1, 0), (1, 0), (1,)]
    for step, colours in enumerate(plan):
        if step > 0:
            iterate = exchange_y(iterate[:, width:width + span_y], width)
        for colour in colours:
            iterate = half_sweep(iterate, source, divisor, weight, allowed, colour)
    return iterate


def x_window(values, start, length, margin):
    padded = jnp.pad(values, ((margin, margin), (0, 0), (0, 0)))
    return lax.dynamic_slice_in_dim(padded, start, length, axis=0)


def dirichlet_kernel(volts_ref, potential_ref, charge_ref, region_ref, packed_ref):
    region = region_ref[...]
    total = jnp.zeros(region.shape, jnp.float32)
    for electrode in range(volts_ref.shape[0]):
        total = total + jnp.where(region == electrode + 1, volts_ref[electrode], jnp.float32(0.0))
    depth = region.shape[2]
    packed_ref[:, :, 0:depth] = potential_ref[...]
    packed_ref[:, :, depth:2 * depth] = charge_ref[...]
    packed_ref[:, :, 2 * depth:3 * depth] = region.astype(jnp.float32)
    packed_ref[:, :, 3 * depth:4 * depth] = total


def packed_inputs(potential, charge, region, electrode_volts):
    span_x, span_y, depth = potential.shape
    vmem = pl.BlockSpec(memory_space=pltpu.VMEM)
    return pl.pallas_call(
        dirichlet_kernel,
        out_shape=jax.ShapeDtypeStruct((span_x, span_y, 4 * depth), jnp.float32),
        in_specs=[pl.BlockSpec(memory_space=pltpu.SMEM), vmem, vmem, vmem],
        out_specs=vmem,
    )(electrode_volts, potential, charge, region)


def body(potential, charge, region, electrode_volts):
    span_x, span_y, depth = potential.shape
    width = HALO_FINE
    packed = exchange(packed_inputs(potential, charge, region, electrode_volts), width)
    potential, charge, region_f, dirichlet = [
        packed[:, :, i * depth:(i + 1) * depth] for i in range(4)
    ]
    movable = jnp.logical_and(region_f == 0.0, inside(span_x, span_y, width))
    flat_sum, vertical = neighbour_sums(pad_plane(potential))
    source = (
        charge - (6.0 * potential - (flat_sum + vertical)) - screen * (jnp.exp(potential) - 1.0)
    )
    coefficient = screen * jnp.exp(potential)
    divisor = 4.0 * 1.0 + 2.0 + coefficient
    iterate = sweeps(dirichlet, source, divisor, 1.0, movable, 1)
    residual = residual_of(iterate, source, divisor, 1.0, movable)
    source_1 = restrict(residual, width, width, span_x, span_y)
    coefficient_1 = coarsen(interior(coefficient, width))

    level_1 = descend(1, source_1, coefficient_1, HALO_MID)
    source_2, coefficient_2 = level_1[5], level_1[6]
    span_x2 = source_2.shape[0]
    whole = gather_x(jnp.concatenate([source_2, coefficient_2], axis=2))
    level_2 = descend_whole_x(2, whole[:, :, :depth], whole[:, :, depth:], HALO_MID)
    iterate_3 = coarsest_whole_x(level_2[5], level_2[6], HALO_COARSE)

    iterate_2, source_2, divisor_2, weight_2, allowed_2 = level_2[:5]
    iterate_2 = sweeps(iterate_2 + lift(iterate_3), source_2, divisor_2, weight_2, allowed_2, 1)
    rim = HALO_MID // 2
    iterate_2 = exchange_y(iterate_2[:, HALO_MID:HALO_MID + source_2.shape[1] - 2 * HALO_MID], rim)
    iterate_2 = x_window(iterate_2, lax.axis_index("gx") * span_x2, span_x2 + 2 * rim, rim)

    iterate_1, source_1, divisor_1, weight_1, allowed_1 = level_1[:5]
    iterate_1 = sweeps(iterate_1 + lift(iterate_2), source_1, divisor_1, weight_1, allowed_1, 1)
    lifted = lift(interior(iterate_1, HALO_MID // 2))

    iterate = iterate + jnp.where(movable, lifted, 0.0)
    iterate = sweeps(iterate, source, divisor, 1.0, movable, 1)
    return interior(iterate, width)


def solution(mesh):
    placed = (P("gx", "gy", None), P("gx", "gy", None), P("gx", "gy", None), P())
    return jax.shard_map(
        body, mesh=mesh, in_specs=placed, out_specs=P("gx", "gy", None), check_vma=False
    )
```

```python
import jax
import jax.numpy as jnp
from jax import lax
from jax.experimental import pallas as pl
from jax.experimental.pallas import tpu as pltpu
from jax.sharding import PartitionSpec as P

screen = 0.5

HALO_0 = 4
HALO_1 = 14
HALO_2 = 5
HALO_3 = 9


def shifted(block, axis, distance):
    count = lax.axis_size(axis)
    route = [(i, i + distance) for i in range(count) if 0 <= i + distance < count]
    if not route:
        return jnp.zeros_like(block)
    return lax.ppermute(block, axis, route)


def along(block, width, axis, dim):
    span = block.shape[dim]
    reach = -(-width // span)
    part = width - (reach - 1) * span
    low = [shifted(lax.slice_in_dim(block, span - part, span, axis=dim), axis, reach)]
    low += [shifted(block, axis, d) for d in range(reach - 1, 0, -1)]
    high = [shifted(block, axis, -d) for d in range(1, reach)]
    high += [shifted(lax.slice_in_dim(block, 0, part, axis=dim), axis, -reach)]
    return jnp.concatenate(low + [block] + high, axis=dim)


def exchange(block, width):
    return along(along(block, width, "gx", 0), width, "gy", 1)


def exchange_y(block, width):
    return jnp.concatenate(
        [shifted(block[:, -width:], "gy", 1), block, shifted(block[:, :width], "gy", -1)], axis=1
    )


def gather_x(block):
    count, index = lax.axis_size("gx"), lax.axis_index("gx")
    step = 1
    while step < count:
        other = lax.ppermute(block, "gx", [(i, i ^ step) for i in range(count)])
        lower = (index & step) == 0
        block = jnp.where(
            lower, jnp.concatenate([block, other], axis=0), jnp.concatenate([other, block], axis=0)
        )
        step *= 2
    return block


def exchange_many(arrays, width, exchanger=exchange):
    depth = arrays[0].shape[2]
    packed = exchanger(jnp.concatenate(arrays, axis=2), width)
    return [packed[:, :, i * depth:(i + 1) * depth] for i in range(len(arrays))]


def inside(span_x, span_y, width, whole_x=False):
    index_y = lax.axis_index("gy") * span_y - width + jnp.arange(span_y + 2 * width)
    total_y = span_y * lax.axis_size("gy")
    keep_y = (index_y >= 0) & (index_y < total_y)
    if whole_x:
        return jnp.broadcast_to(keep_y[None, :, None], (span_x, span_y + 2 * width, 1))
    index_x = lax.axis_index("gx") * span_x - width + jnp.arange(span_x + 2 * width)
    total_x = span_x * lax.axis_size("gx")
    keep_x = (index_x >= 0) & (index_x < total_x)
    return (keep_x[:, None] & keep_y[None, :])[:, :, None]


def pad_plane(values):
    return jnp.pad(values, ((1, 1), (1, 1), (0, 0)))


def neighbour_sums(padded):
    interior = padded[1:-1, 1:-1]
    flat_sum = padded[2:, 1:-1] + padded[:-2, 1:-1] + padded[1:-1, 2:] + padded[1:-1, :-2]
    padded_z = jnp.pad(interior, ((0, 0), (0, 0), (1, 1)))
    vertical = padded_z[:, :, 2:] + padded_z[:, :, :-2]
    return (flat_sum, vertical)


def checker(span_x, span_y, span_z):
    index_x = jnp.arange(span_x, dtype=jnp.int32)[:, None, None]
    index_y = jnp.arange(span_y, dtype=jnp.int32)[None, :, None]
    index_z = jnp.arange(span_z, dtype=jnp.int32)[None, None, :]
    return (index_x + index_y + index_z) % 2


def half_sweep(iterate, source, divisor, weight, allowed, colour):
    flat_sum, vertical = neighbour_sums(pad_plane(iterate))
    renewed = (source + weight * flat_sum + vertical) / divisor
    span_x, span_y, span_z = iterate.shape
    update = jnp.logical_and(checker(span_x, span_y, span_z) == colour, allowed)
    return jnp.where(update, renewed, iterate)


def sweeps(iterate, source, divisor, weight, allowed, count):
    for _ in range(count):
        iterate = half_sweep(iterate, source, divisor, weight, allowed, 0)
        iterate = half_sweep(iterate, source, divisor, weight, allowed, 1)
    return iterate


def residual_of(iterate, source, divisor, weight, allowed):
    flat_sum, vertical = neighbour_sums(pad_plane(iterate))
    residual = source - (divisor * iterate - (weight * flat_sum + vertical))
    return jnp.where(allowed, residual, 0.0)


def restrict(values, width, rim, span_x, span_y):
    low = width - 2 * rim - 1
    rows = values[low:width + span_x + 2 * rim]
    count = span_x // 2 + 2 * rim
    before = rows[:-1].reshape(count, 2, *rows.shape[1:])[:, 0]
    paired = rows[1:].reshape(count, 2, *rows.shape[1:])
    across = 0.25 * before + 0.5 * paired[:, 0] + 0.25 * paired[:, 1]
    cols = across[:, low:width + span_y + 2 * rim]
    count_y = span_y // 2 + 2 * rim
    before = cols[:, :-1].reshape(count, count_y, 2, cols.shape[2])[:, :, 0]
    paired = cols[:, 1:].reshape(count, count_y, 2, cols.shape[2])
    return 0.25 * before + 0.5 * paired[:, :, 0] + 0.25 * paired[:, :, 1]


def coarsen(values):
    paired = values.reshape(values.shape[0] // 2, 2, values.shape[1], values.shape[2])
    across = 0.5 * (paired[:, 0] + paired[:, 1])
    paired = across.reshape(across.shape[0], across.shape[1] // 2, 2, across.shape[2])
    return 0.5 * (paired[:, :, 0] + paired[:, :, 1])


def lift(coarse):
    return jnp.repeat(jnp.repeat(coarse, 2, axis=0), 2, axis=1)


def interior(values, width):
    return values[width:values.shape[0] - width, width:values.shape[1] - width]


def trimmed(values, cut):
    return values[cut:values.shape[0] - cut, cut:values.shape[1] - cut]


def dirichlet_kernel(volts_ref, potential_ref, charge_ref, region_ref, packed_ref):
    region = region_ref[...]
    total = jnp.zeros(region.shape, jnp.float32)
    for electrode in range(volts_ref.shape[0]):
        total = total + jnp.where(region == electrode + 1, volts_ref[electrode], jnp.float32(0.0))
    depth = region.shape[2]
    packed_ref[:, :, 0:depth] = potential_ref[...]
    packed_ref[:, :, depth:2 * depth] = charge_ref[...]
    packed_ref[:, :, 2 * depth:3 * depth] = region.astype(jnp.float32)
    packed_ref[:, :, 3 * depth:4 * depth] = total


def packed_inputs(potential, charge, region, electrode_volts):
    span_x, span_y, depth = potential.shape
    vmem = pl.BlockSpec(memory_space=pltpu.VMEM)
    return pl.pallas_call(
        dirichlet_kernel,
        out_shape=jax.ShapeDtypeStruct((span_x, span_y, 4 * depth), jnp.float32),
        in_specs=[pl.BlockSpec(memory_space=pltpu.SMEM), vmem, vmem, vmem],
        out_specs=vmem,
    )(electrode_volts, potential, charge, region)


def body(potential, charge, region, electrode_volts):
    span_x, span_y, depth = potential.shape
    packed = exchange(packed_inputs(potential, charge, region, electrode_volts), HALO_0)
    potential, charge, region_f, dirichlet = [
        packed[:, :, i * depth:(i + 1) * depth] for i in range(4)
    ]
    movable = jnp.logical_and(region_f == 0.0, inside(span_x, span_y, HALO_0))
    flat_sum, vertical = neighbour_sums(pad_plane(potential))
    source_0 = (
        charge - (6.0 * potential - (flat_sum + vertical)) - screen * (jnp.exp(potential) - 1.0)
    )
    coefficient_0 = screen * jnp.exp(potential)
    divisor_0 = 4.0 * 1.0 + 2.0 + coefficient_0
    iterate_0 = sweeps(dirichlet, source_0, divisor_0, 1.0, movable, 1)
    residual = residual_of(iterate_0, source_0, divisor_0, 1.0, movable)
    source_1 = restrict(residual, HALO_0, 0, span_x, span_y)
    coefficient_1 = coarsen(interior(coefficient_0, HALO_0))

    span_x1, span_y1 = span_x // 2, span_y // 2
    source_1, coefficient_1 = exchange_many([source_1, coefficient_1], HALO_1)
    weight_1 = 0.25
    divisor_1 = 4.0 * weight_1 + 2.0 + coefficient_1
    allowed_1 = inside(span_x1, span_y1, HALO_1)
    iterate_1 = sweeps(jnp.zeros_like(source_1), source_1, divisor_1, weight_1, allowed_1, 1)
    residual = residual_of(iterate_1, source_1, divisor_1, weight_1, allowed_1)
    source_2 = restrict(residual, HALO_1, HALO_2, span_x1, span_y1)
    keep = HALO_1 - 2 * HALO_2
    coefficient_2 = coarsen(trimmed(coefficient_1, keep))

    span_x2, span_y2 = span_x1 // 2, span_y1 // 2
    weight_2 = 0.25**2
    divisor_2 = 4.0 * weight_2 + 2.0 + coefficient_2
    allowed_2 = inside(span_x2, span_y2, HALO_2)
    iterate_2 = sweeps(jnp.zeros_like(source_2), source_2, divisor_2, weight_2, allowed_2, 1)
    residual = residual_of(iterate_2, source_2, divisor_2, weight_2, allowed_2)
    source_3 = restrict(residual, HALO_2, 0, span_x2, span_y2)
    coefficient_3 = coarsen(interior(coefficient_2, HALO_2))

    span_x3, span_y3 = span_x2 // 2, span_y2 // 2
    source_3, coefficient_3 = exchange_many([source_3, coefficient_3], HALO_3)
    weight_3 = 0.25**3
    divisor_3 = 4.0 * weight_3 + 2.0 + coefficient_3
    allowed_3 = inside(span_x3, span_y3, HALO_3)
    iterate_3 = sweeps(jnp.zeros_like(source_3), source_3, divisor_3, weight_3, allowed_3, 4)

    cut = HALO_2 - 4
    iterate_2 = trimmed(iterate_2, cut) + lift(trimmed(iterate_3, HALO_3 - 2))
    iterate_2 = sweeps(
        iterate_2, trimmed(source_2, cut), trimmed(divisor_2, cut), weight_2, trimmed(allowed_2, cut), 1
    )
    cut = HALO_1 - 4
    iterate_1 = trimmed(iterate_1, cut) + lift(trimmed(iterate_2, 2))
    iterate_1 = sweeps(
        iterate_1, trimmed(source_1, cut), trimmed(divisor_1, cut), weight_1, trimmed(allowed_1, cut), 1
    )
    lifted = lift(trimmed(iterate_1, 2))
    iterate_0 = iterate_0 + jnp.where(movable, lifted, 0.0)
    iterate_0 = sweeps(iterate_0, source_0, divisor_0, 1.0, movable, 1)
    return interior(iterate_0, HALO_0)


def solution(mesh):
    placed = (P("gx", "gy", None), P("gx", "gy", None), P("gx", "gy", None), P())
    return jax.shard_map(
        body, mesh=mesh, in_specs=placed, out_specs=P("gx", "gy", None), check_vma=False
    )
```

```python
import jax
import jax.numpy as jnp
from jax import lax
from jax.experimental import pallas as pl
from jax.experimental.pallas import tpu as pltpu
from jax.sharding import PartitionSpec as P

screen = 0.5

HALO_FINE = 4
HALO_MID = 4
HALO_COARSE = 2


def shifted(block, axis, distance):
    count = lax.axis_size(axis)
    route = [(i, i + distance) for i in range(count) if 0 <= i + distance < count]
    return lax.ppermute(block, axis, route)


def exchange(block, width):
    block = jnp.concatenate(
        [shifted(block[-width:], "gx", 1), block, shifted(block[:width], "gx", -1)], axis=0
    )
    return jnp.concatenate(
        [shifted(block[:, -width:], "gy", 1), block, shifted(block[:, :width], "gy", -1)], axis=1
    )


def exchange_y(block, width):
    return jnp.concatenate(
        [shifted(block[:, -width:], "gy", 1), block, shifted(block[:, :width], "gy", -1)], axis=1
    )


def gather_x(block):
    count, index = lax.axis_size("gx"), lax.axis_index("gx")
    group = 1
    while group < count:
        size = min(4, count // group)
        received = [block] + [
            lax.ppermute(block, "gx", [(i, i ^ (m * group)) for i in range(count)])
            for m in range(1, size)
        ]
        stacked = jnp.stack(received)
        own = (index // group) % size
        block = jnp.concatenate(
            [lax.dynamic_index_in_dim(stacked, q ^ own, keepdims=False) for q in range(size)], axis=0
        )
        group *= size
    return block


def exchange_many(arrays, width, exchanger=exchange):
    depth = arrays[0].shape[2]
    packed = exchanger(jnp.concatenate(arrays, axis=2), width)
    return [packed[:, :, i * depth:(i + 1) * depth] for i in range(len(arrays))]


def inside(span_x, span_y, width, whole_x=False):
    index_y = lax.axis_index("gy") * span_y - width + jnp.arange(span_y + 2 * width)
    total_y = span_y * lax.axis_size("gy")
    keep_y = (index_y >= 0) & (index_y < total_y)
    if whole_x:
        return jnp.broadcast_to(keep_y[None, :, None], (span_x, span_y + 2 * width, 1))
    index_x = lax.axis_index("gx") * span_x - width + jnp.arange(span_x + 2 * width)
    total_x = span_x * lax.axis_size("gx")
    keep_x = (index_x >= 0) & (index_x < total_x)
    return (keep_x[:, None] & keep_y[None, :])[:, :, None]


def pad_plane(values):
    return jnp.pad(values, ((1, 1), (1, 1), (0, 0)))


def neighbour_sums(padded):
    interior = padded[1:-1, 1:-1]
    flat_sum = padded[2:, 1:-1] + padded[:-2, 1:-1] + padded[1:-1, 2:] + padded[1:-1, :-2]
    padded_z = jnp.pad(interior, ((0, 0), (0, 0), (1, 1)))
    vertical = padded_z[:, :, 2:] + padded_z[:, :, :-2]
    return (flat_sum, vertical)


def checker(span_x, span_y, span_z):
    index_x = jnp.arange(span_x, dtype=jnp.int32)[:, None, None]
    index_y = jnp.arange(span_y, dtype=jnp.int32)[None, :, None]
    index_z = jnp.arange(span_z, dtype=jnp.int32)[None, None, :]
    return (index_x + index_y + index_z) % 2


def half_sweep(iterate, source, divisor, weight, allowed, colour):
    flat_sum, vertical = neighbour_sums(pad_plane(iterate))
    renewed = (source + weight * flat_sum + vertical) / divisor
    span_x, span_y, span_z = iterate.shape
    update = jnp.logical_and(checker(span_x, span_y, span_z) == colour, allowed)
    return jnp.where(update, renewed, iterate)


def sweeps(iterate, source, divisor, weight, allowed, count):
    for _ in range(count):
        iterate = half_sweep(iterate, source, divisor, weight, allowed, 0)
        iterate = half_sweep(iterate, source, divisor, weight, allowed, 1)
    return iterate


def residual_of(iterate, source, divisor, weight, allowed):
    flat_sum, vertical = neighbour_sums(pad_plane(iterate))
    residual = source - (divisor * iterate - (weight * flat_sum + vertical))
    return jnp.where(allowed, residual, 0.0)


def restrict(values, width_x, width_y, span_x, span_y):
    rows = values[width_x - 1:width_x + span_x]
    before = rows[:-1].reshape(span_x // 2, 2, *rows.shape[1:])[:, 0]
    paired = rows[1:].reshape(span_x // 2, 2, *rows.shape[1:])
    across = 0.25 * before + 0.5 * paired[:, 0] + 0.25 * paired[:, 1]
    cols = across[:, width_y - 1:width_y + span_y]
    before = cols[:, :-1].reshape(cols.shape[0], span_y // 2, 2, cols.shape[2])[:, :, 0]
    paired = cols[:, 1:].reshape(cols.shape[0], span_y // 2, 2, cols.shape[2])
    return 0.25 * before + 0.5 * paired[:, :, 0] + 0.25 * paired[:, :, 1]


def coarsen(values):
    paired = values.reshape(values.shape[0] // 2, 2, values.shape[1], values.shape[2])
    across = 0.5 * (paired[:, 0] + paired[:, 1])
    paired = across.reshape(across.shape[0], across.shape[1] // 2, 2, across.shape[2])
    return 0.5 * (paired[:, :, 0] + paired[:, :, 1])


def lift(coarse):
    return jnp.repeat(jnp.repeat(coarse, 2, axis=0), 2, axis=1)


def interior(values, width):
    return values[width:values.shape[0] - width, width:values.shape[1] - width]


def descend(grid_level, source, coefficient, width):
    span_x, span_y = source.shape[0], source.shape[1]
    source, coefficient_ext = exchange_many([source, coefficient], width)
    weight = 0.25**grid_level
    divisor = 4.0 * weight + 2.0 + coefficient_ext
    allowed = inside(span_x, span_y, width)
    iterate = sweeps(jnp.zeros_like(source), source, divisor, weight, allowed, 1)
    residual = residual_of(iterate, source, divisor, weight, allowed)
    coarse_source = restrict(residual, width, width, span_x, span_y)
    coarse_coefficient = coarsen(interior(coefficient_ext, width))
    return iterate, source, divisor, weight, allowed, coarse_source, coarse_coefficient


def descend_whole_x(grid_level, source, coefficient, width):
    span_y = source.shape[1]
    source, coefficient = exchange_many([source, coefficient], width, exchange_y)
    span_x = source.shape[0]
    weight = 0.25**grid_level
    divisor = 4.0 * weight + 2.0 + coefficient
    allowed = inside(span_x, span_y, width, whole_x=True)
    iterate = sweeps(jnp.zeros_like(source), source, divisor, weight, allowed, 1)
    residual = residual_of(iterate, source, divisor, weight, allowed)
    residual = jnp.pad(residual, ((1, 0), (0, 0), (0, 0)))
    coarse_source = restrict(residual, 1, width, span_x, span_y)
    coarse_coefficient = coarsen(coefficient[:, width:width + span_y])
    return iterate, source, divisor, weight, allowed, coarse_source, coarse_coefficient


def coarsest_whole_x(source, coefficient, width):
    span_y = source.shape[1]
    source, coefficient = exchange_many([source, coefficient], width, exchange_y)
    span_x = source.shape[0]
    weight = 0.25**3
    divisor = 4.0 * weight + 2.0 + coefficient
    allowed = inside(span_x, span_y, width, whole_x=True)
    iterate = jnp.zeros_like(source)
    plan = [(0, 1, 0), (1, 0), (1, 0), (1,)]
    for step, colours in enumerate(plan):
        if step > 0:
            iterate = exchange_y(iterate[:, width:width + span_y], width)
        for colour in colours:
            iterate = half_sweep(iterate, source, divisor, weight, allowed, colour)
    return iterate


def x_window(values, start, length, margin):
    padded = jnp.pad(values, ((margin, margin), (0, 0), (0, 0)))
    return lax.dynamic_slice_in_dim(padded, start, length, axis=0)


def dirichlet_kernel(volts_ref, potential_ref, charge_ref, region_ref, packed_ref):
    region = region_ref[...]
    total = jnp.zeros(region.shape, jnp.float32)
    for electrode in range(volts_ref.shape[0]):
        total = total + jnp.where(region == electrode + 1, volts_ref[electrode], jnp.float32(0.0))
    depth = region.shape[2]
    packed_ref[:, :, 0:depth] = potential_ref[...]
    packed_ref[:, :, depth:2 * depth] = charge_ref[...]
    packed_ref[:, :, 2 * depth:3 * depth] = region.astype(jnp.float32)
    packed_ref[:, :, 3 * depth:4 * depth] = total


def packed_inputs(potential, charge, region, electrode_volts):
    span_x, span_y, depth = potential.shape
    vmem = pl.BlockSpec(memory_space=pltpu.VMEM)
    return pl.pallas_call(
        dirichlet_kernel,
        out_shape=jax.ShapeDtypeStruct((span_x, span_y, 4 * depth), jnp.float32),
        in_specs=[pl.BlockSpec(memory_space=pltpu.SMEM), vmem, vmem, vmem],
        out_specs=vmem,
    )(electrode_volts, potential, charge, region)


def body(potential, charge, region, electrode_volts):
    span_x, span_y, depth = potential.shape
    width = HALO_FINE
    packed = exchange(packed_inputs(potential, charge, region, electrode_volts), width)
    potential, charge, region_f, dirichlet = [
        packed[:, :, i * depth:(i + 1) * depth] for i in range(4)
    ]
    movable = jnp.logical_and(region_f == 0.0, inside(span_x, span_y, width))
    flat_sum, vertical = neighbour_sums(pad_plane(potential))
    source = (
        charge - (6.0 * potential - (flat_sum + vertical)) - screen * (jnp.exp(potential) - 1.0)
    )
    coefficient = screen * jnp.exp(potential)
    divisor = 4.0 * 1.0 + 2.0 + coefficient
    iterate = sweeps(dirichlet, source, divisor, 1.0, movable, 1)
    residual = residual_of(iterate, source, divisor, 1.0, movable)
    source_1 = restrict(residual, width, width, span_x, span_y)
    coefficient_1 = coarsen(interior(coefficient, width))

    level_1 = descend(1, source_1, coefficient_1, HALO_MID)
    source_2, coefficient_2 = level_1[5], level_1[6]
    span_x2 = source_2.shape[0]
    whole = gather_x(jnp.concatenate([source_2, coefficient_2], axis=2))
    level_2 = descend_whole_x(2, whole[:, :, :depth], whole[:, :, depth:], HALO_MID)
    iterate_3 = coarsest_whole_x(level_2[5], level_2[6], HALO_COARSE)

    iterate_2, source_2, divisor_2, weight_2, allowed_2 = level_2[:5]
    iterate_2 = sweeps(iterate_2 + lift(iterate_3), source_2, divisor_2, weight_2, allowed_2, 1)
    rim = HALO_MID // 2
    iterate_2 = exchange_y(iterate_2[:, HALO_MID:HALO_MID + source_2.shape[1] - 2 * HALO_MID], rim)
    iterate_2 = x_window(iterate_2, lax.axis_index("gx") * span_x2, span_x2 + 2 * rim, rim)

    iterate_1, source_1, divisor_1, weight_1, allowed_1 = level_1[:5]
    iterate_1 = sweeps(iterate_1 + lift(iterate_2), source_1, divisor_1, weight_1, allowed_1, 1)
    lifted = lift(interior(iterate_1, HALO_MID // 2))

    iterate = iterate + jnp.where(movable, lifted, 0.0)
    iterate = sweeps(iterate, source, divisor, 1.0, movable, 1)
    return interior(iterate, width)


def solution(mesh):
    placed = (P("gx", "gy", None), P("gx", "gy", None), P("gx", "gy", None), P())
    return jax.shard_map(
        body, mesh=mesh, in_specs=placed, out_specs=P("gx", "gy", None), check_vma=False
    )
```

```python
import jax
import jax.numpy as jnp
from jax import lax
from jax.experimental import pallas as pl
from jax.experimental.pallas import tpu as pltpu
from jax.sharding import PartitionSpec as P

screen = 0.5

HALO_FINE = 4
HALO_MID = 4
HALO_COARSE = 4


def shifted(block, axis, distance):
    count = lax.axis_size(axis)
    route = [(i, i + distance) for i in range(count) if 0 <= i + distance < count]
    if not route:
        return jnp.zeros_like(block)
    return lax.ppermute(block, axis, route)


def exchange(block, width):
    block = jnp.concatenate(
        [shifted(block[-width:], "gx", 1), block, shifted(block[:width], "gx", -1)], axis=0
    )
    return jnp.concatenate(
        [shifted(block[:, -width:], "gy", 1), block, shifted(block[:, :width], "gy", -1)], axis=1
    )


def along(block, width, axis, dim):
    span = block.shape[dim]
    reach = -(-width // span)
    part = width - (reach - 1) * span
    low = [shifted(lax.slice_in_dim(block, span - part, span, axis=dim), axis, reach)]
    low += [shifted(block, axis, d) for d in range(reach - 1, 0, -1)]
    high = [shifted(block, axis, -d) for d in range(1, reach)]
    high += [shifted(lax.slice_in_dim(block, 0, part, axis=dim), axis, -reach)]
    return jnp.concatenate(low + [block] + high, axis=dim)


def exchange_y(block, width):
    return jnp.concatenate(
        [shifted(block[:, -width:], "gy", 1), block, shifted(block[:, :width], "gy", -1)], axis=1
    )


def gather_x(block):
    count, index = lax.axis_size("gx"), lax.axis_index("gx")
    group = 1
    while group < count:
        size = min(4, count // group)
        received = [block] + [
            lax.ppermute(block, "gx", [(i, i ^ (m * group)) for i in range(count)])
            for m in range(1, size)
        ]
        stacked = jnp.stack(received)
        own = (index // group) % size
        block = jnp.concatenate(
            [lax.dynamic_index_in_dim(stacked, q ^ own, keepdims=False) for q in range(size)], axis=0
        )
        group *= size
    return block


def exchange_many(arrays, width, exchanger=exchange):
    depth = arrays[0].shape[2]
    packed = exchanger(jnp.concatenate(arrays, axis=2), width)
    return [packed[:, :, i * depth:(i + 1) * depth] for i in range(len(arrays))]


def inside(span_x, span_y, width, whole_x=False):
    index_y = lax.axis_index("gy") * span_y - width + jnp.arange(span_y + 2 * width)
    total_y = span_y * lax.axis_size("gy")
    keep_y = (index_y >= 0) & (index_y < total_y)
    if whole_x:
        return jnp.broadcast_to(keep_y[None, :, None], (span_x, span_y + 2 * width, 1))
    index_x = lax.axis_index("gx") * span_x - width + jnp.arange(span_x + 2 * width)
    total_x = span_x * lax.axis_size("gx")
    keep_x = (index_x >= 0) & (index_x < total_x)
    return (keep_x[:, None] & keep_y[None, :])[:, :, None]


def pad_plane(values):
    return jnp.pad(values, ((1, 1), (1, 1), (0, 0)))


def neighbour_sums(padded):
    interior = padded[1:-1, 1:-1]
    flat_sum = padded[2:, 1:-1] + padded[:-2, 1:-1] + padded[1:-1, 2:] + padded[1:-1, :-2]
    padded_z = jnp.pad(interior, ((0, 0), (0, 0), (1, 1)))
    vertical = padded_z[:, :, 2:] + padded_z[:, :, :-2]
    return (flat_sum, vertical)


def checker(span_x, span_y, span_z):
    index_x = jnp.arange(span_x, dtype=jnp.int32)[:, None, None]
    index_y = jnp.arange(span_y, dtype=jnp.int32)[None, :, None]
    index_z = jnp.arange(span_z, dtype=jnp.int32)[None, None, :]
    return (index_x + index_y + index_z) % 2


def half_sweep(iterate, source, divisor, weight, allowed, colour):
    flat_sum, vertical = neighbour_sums(pad_plane(iterate))
    renewed = (source + weight * flat_sum + vertical) / divisor
    span_x, span_y, span_z = iterate.shape
    update = jnp.logical_and(checker(span_x, span_y, span_z) == colour, allowed)
    return jnp.where(update, renewed, iterate)


def sweeps(iterate, source, divisor, weight, allowed, count):
    for _ in range(count):
        iterate = half_sweep(iterate, source, divisor, weight, allowed, 0)
        iterate = half_sweep(iterate, source, divisor, weight, allowed, 1)
    return iterate


def residual_of(iterate, source, divisor, weight, allowed):
    flat_sum, vertical = neighbour_sums(pad_plane(iterate))
    residual = source - (divisor * iterate - (weight * flat_sum + vertical))
    return jnp.where(allowed, residual, 0.0)


def restrict(values, width_x, width_y, span_x, span_y):
    rows = values[width_x - 1:width_x + span_x]
    before = rows[:-1].reshape(span_x // 2, 2, *rows.shape[1:])[:, 0]
    paired = rows[1:].reshape(span_x // 2, 2, *rows.shape[1:])
    across = 0.25 * before + 0.5 * paired[:, 0] + 0.25 * paired[:, 1]
    cols = across[:, width_y - 1:width_y + span_y]
    before = cols[:, :-1].reshape(cols.shape[0], span_y // 2, 2, cols.shape[2])[:, :, 0]
    paired = cols[:, 1:].reshape(cols.shape[0], span_y // 2, 2, cols.shape[2])
    return 0.25 * before + 0.5 * paired[:, :, 0] + 0.25 * paired[:, :, 1]


def coarsen(values):
    paired = values.reshape(values.shape[0] // 2, 2, values.shape[1], values.shape[2])
    across = 0.5 * (paired[:, 0] + paired[:, 1])
    paired = across.reshape(across.shape[0], across.shape[1] // 2, 2, across.shape[2])
    return 0.5 * (paired[:, :, 0] + paired[:, :, 1])


def lift(coarse):
    return jnp.repeat(jnp.repeat(coarse, 2, axis=0), 2, axis=1)


def interior(values, width):
    return values[width:values.shape[0] - width, width:values.shape[1] - width]


def descend(grid_level, source, coefficient, width):
    span_x, span_y = source.shape[0], source.shape[1]
    source, coefficient_ext = exchange_many([source, coefficient], width)
    weight = 0.25**grid_level
    divisor = 4.0 * weight + 2.0 + coefficient_ext
    allowed = inside(span_x, span_y, width)
    iterate = sweeps(jnp.zeros_like(source), source, divisor, weight, allowed, 1)
    residual = residual_of(iterate, source, divisor, weight, allowed)
    coarse_source = restrict(residual, width, width, span_x, span_y)
    coarse_coefficient = coarsen(interior(coefficient_ext, width))
    return iterate, source, divisor, weight, allowed, coarse_source, coarse_coefficient


def descend_whole_x(grid_level, source, coefficient, width):
    span_y = source.shape[1]
    source, coefficient = exchange_many([source, coefficient], width, exchange_y)
    span_x = source.shape[0]
    weight = 0.25**grid_level
    divisor = 4.0 * weight + 2.0 + coefficient
    allowed = inside(span_x, span_y, width, whole_x=True)
    iterate = sweeps(jnp.zeros_like(source), source, divisor, weight, allowed, 1)
    residual = residual_of(iterate, source, divisor, weight, allowed)
    residual = jnp.pad(residual, ((1, 0), (0, 0), (0, 0)))
    coarse_source = restrict(residual, 1, width, span_x, span_y)
    coarse_coefficient = coarsen(coefficient[:, width:width + span_y])
    return iterate, source, divisor, weight, allowed, coarse_source, coarse_coefficient


def coarsest_whole_x(source, coefficient, width):
    span_y = source.shape[1]
    exchanger = lambda block, rim: along(block, rim, "gy", 1)
    source, coefficient = exchange_many([source, coefficient], width, exchanger)
    span_x = source.shape[0]
    weight = 0.25**3
    divisor = 4.0 * weight + 2.0 + coefficient
    allowed = inside(span_x, span_y, width, whole_x=True)
    iterate = jnp.zeros_like(source)
    plan = [(0, 1, 0, 1, 0), (1, 0, 1)]
    for step, colours in enumerate(plan):
        if step > 0:
            iterate = exchanger(iterate[:, width:width + span_y], width)
        for colour in colours:
            iterate = half_sweep(iterate, source, divisor, weight, allowed, colour)
    cut = width - 2
    return iterate[:, cut:iterate.shape[1] - cut]


def x_window(values, start, length, margin):
    padded = jnp.pad(values, ((margin, margin), (0, 0), (0, 0)))
    return lax.dynamic_slice_in_dim(padded, start, length, axis=0)


def dirichlet_kernel(volts_ref, potential_ref, charge_ref, region_ref, packed_ref):
    region = region_ref[...]
    total = jnp.zeros(region.shape, jnp.float32)
    for electrode in range(volts_ref.shape[0]):
        total = total + jnp.where(region == electrode + 1, volts_ref[electrode], jnp.float32(0.0))
    depth = region.shape[2]
    packed_ref[:, :, 0:depth] = potential_ref[...]
    packed_ref[:, :, depth:2 * depth] = charge_ref[...]
    packed_ref[:, :, 2 * depth:3 * depth] = region.astype(jnp.float32)
    packed_ref[:, :, 3 * depth:4 * depth] = total


def packed_inputs(potential, charge, region, electrode_volts):
    span_x, span_y, depth = potential.shape
    vmem = pl.BlockSpec(memory_space=pltpu.VMEM)
    return pl.pallas_call(
        dirichlet_kernel,
        out_shape=jax.ShapeDtypeStruct((span_x, span_y, 4 * depth), jnp.float32),
        in_specs=[pl.BlockSpec(memory_space=pltpu.SMEM), vmem, vmem, vmem],
        out_specs=vmem,
    )(electrode_volts, potential, charge, region)


def body(potential, charge, region, electrode_volts):
    span_x, span_y, depth = potential.shape
    width = HALO_FINE
    packed = exchange(packed_inputs(potential, charge, region, electrode_volts), width)
    potential, charge, region_f, dirichlet = [
        packed[:, :, i * depth:(i + 1) * depth] for i in range(4)
    ]
    movable = jnp.logical_and(region_f == 0.0, inside(span_x, span_y, width))
    flat_sum, vertical = neighbour_sums(pad_plane(potential))
    source = (
        charge - (6.0 * potential - (flat_sum + vertical)) - screen * (jnp.exp(potential) - 1.0)
    )
    coefficient = screen * jnp.exp(potential)
    divisor = 4.0 * 1.0 + 2.0 + coefficient
    iterate = sweeps(dirichlet, source, divisor, 1.0, movable, 1)
    residual = residual_of(iterate, source, divisor, 1.0, movable)
    source_1 = restrict(residual, width, width, span_x, span_y)
    coefficient_1 = coarsen(interior(coefficient, width))

    level_1 = descend(1, source_1, coefficient_1, HALO_MID)
    source_2, coefficient_2 = level_1[5], level_1[6]
    span_x2 = source_2.shape[0]
    whole = gather_x(jnp.concatenate([source_2, coefficient_2], axis=2))
    level_2 = descend_whole_x(2, whole[:, :, :depth], whole[:, :, depth:], HALO_MID)
    iterate_3 = coarsest_whole_x(level_2[5], level_2[6], HALO_COARSE)

    iterate_2, source_2, divisor_2, weight_2, allowed_2 = level_2[:5]
    iterate_2 = sweeps(iterate_2 + lift(iterate_3), source_2, divisor_2, weight_2, allowed_2, 1)
    rim = HALO_MID // 2
    iterate_2 = exchange_y(iterate_2[:, HALO_MID:HALO_MID + source_2.shape[1] - 2 * HALO_MID], rim)
    iterate_2 = x_window(iterate_2, lax.axis_index("gx") * span_x2, span_x2 + 2 * rim, rim)

    iterate_1, source_1, divisor_1, weight_1, allowed_1 = level_1[:5]
    iterate_1 = sweeps(iterate_1 + lift(iterate_2), source_1, divisor_1, weight_1, allowed_1, 1)
    lifted = lift(interior(iterate_1, HALO_MID // 2))

    iterate = iterate + jnp.where(movable, lifted, 0.0)
    iterate = sweeps(iterate, source, divisor, 1.0, movable, 1)
    return interior(iterate, width)


def solution(mesh):
    placed = (P("gx", "gy", None), P("gx", "gy", None), P("gx", "gy", None), P())
    return jax.shard_map(
        body, mesh=mesh, in_specs=placed, out_specs=P("gx", "gy", None), check_vma=False
    )
```

```python
import jax
import jax.numpy as jnp
from jax import lax
from jax.experimental import pallas as pl
from jax.experimental.pallas import tpu as pltpu
from jax.sharding import PartitionSpec as P

screen = 0.5

HALO_FINE = 4
HALO_MID = 4
HALO_COARSE = 4
HALO_1_Y = 12


def shifted(block, axis, distance):
    count = lax.axis_size(axis)
    route = [(i, i + distance) for i in range(count) if 0 <= i + distance < count]
    if not route:
        return jnp.zeros_like(block)
    return lax.ppermute(block, axis, route)


def exchange(block, width):
    block = jnp.concatenate(
        [shifted(block[-width:], "gx", 1), block, shifted(block[:width], "gx", -1)], axis=0
    )
    return jnp.concatenate(
        [shifted(block[:, -width:], "gy", 1), block, shifted(block[:, :width], "gy", -1)], axis=1
    )


def along(block, width, axis, dim):
    span = block.shape[dim]
    reach = -(-width // span)
    part = width - (reach - 1) * span
    low = [shifted(lax.slice_in_dim(block, span - part, span, axis=dim), axis, reach)]
    low += [shifted(block, axis, d) for d in range(reach - 1, 0, -1)]
    high = [shifted(block, axis, -d) for d in range(1, reach)]
    high += [shifted(lax.slice_in_dim(block, 0, part, axis=dim), axis, -reach)]
    return jnp.concatenate(low + [block] + high, axis=dim)


def exchange_y(block, width):
    return jnp.concatenate(
        [shifted(block[:, -width:], "gy", 1), block, shifted(block[:, :width], "gy", -1)], axis=1
    )


def gather_x(block):
    count, index = lax.axis_size("gx"), lax.axis_index("gx")
    group = 1
    while group < count:
        size = min(4, count // group)
        received = [block] + [
            lax.ppermute(block, "gx", [(i, i ^ (m * group)) for i in range(count)])
            for m in range(1, size)
        ]
        stacked = jnp.stack(received)
        own = (index // group) % size
        block = jnp.concatenate(
            [lax.dynamic_index_in_dim(stacked, q ^ own, keepdims=False) for q in range(size)], axis=0
        )
        group *= size
    return block


def exchange_many(arrays, width, exchanger=exchange):
    depth = arrays[0].shape[2]
    packed = exchanger(jnp.concatenate(arrays, axis=2), width)
    return [packed[:, :, i * depth:(i + 1) * depth] for i in range(len(arrays))]


def inside(span_x, span_y, width, whole_x=False, width_y=None):
    if width_y is None:
        width_y = width
    index_y = lax.axis_index("gy") * span_y - width_y + jnp.arange(span_y + 2 * width_y)
    total_y = span_y * lax.axis_size("gy")
    keep_y = (index_y >= 0) & (index_y < total_y)
    if whole_x:
        return jnp.broadcast_to(keep_y[None, :, None], (span_x, span_y + 2 * width_y, 1))
    index_x = lax.axis_index("gx") * span_x - width + jnp.arange(span_x + 2 * width)
    total_x = span_x * lax.axis_size("gx")
    keep_x = (index_x >= 0) & (index_x < total_x)
    return (keep_x[:, None] & keep_y[None, :])[:, :, None]


def pad_plane(values):
    return jnp.pad(values, ((1, 1), (1, 1), (0, 0)))


def neighbour_sums(padded):
    interior = padded[1:-1, 1:-1]
    flat_sum = padded[2:, 1:-1] + padded[:-2, 1:-1] + padded[1:-1, 2:] + padded[1:-1, :-2]
    padded_z = jnp.pad(interior, ((0, 0), (0, 0), (1, 1)))
    vertical = padded_z[:, :, 2:] + padded_z[:, :, :-2]
    return (flat_sum, vertical)


def checker(span_x, span_y, span_z):
    index_x = jnp.arange(span_x, dtype=jnp.int32)[:, None, None]
    index_y = jnp.arange(span_y, dtype=jnp.int32)[None, :, None]
    index_z = jnp.arange(span_z, dtype=jnp.int32)[None, None, :]
    return (index_x + index_y + index_z) % 2


def half_sweep(iterate, source, divisor, weight, allowed, colour):
    flat_sum, vertical = neighbour_sums(pad_plane(iterate))
    renewed = (source + weight * flat_sum + vertical) / divisor
    span_x, span_y, span_z = iterate.shape
    update = jnp.logical_and(checker(span_x, span_y, span_z) == colour, allowed)
    return jnp.where(update, renewed, iterate)


def sweeps(iterate, source, divisor, weight, allowed, count):
    for _ in range(count):
        iterate = half_sweep(iterate, source, divisor, weight, allowed, 0)
        iterate = half_sweep(iterate, source, divisor, weight, allowed, 1)
    return iterate


def residual_of(iterate, source, divisor, weight, allowed):
    flat_sum, vertical = neighbour_sums(pad_plane(iterate))
    residual = source - (divisor * iterate - (weight * flat_sum + vertical))
    return jnp.where(allowed, residual, 0.0)


def restrict(values, width_x, width_y, span_x, span_y, rim_y=0):
    rows = values[width_x - 1:width_x + span_x]
    before = rows[:-1].reshape(span_x // 2, 2, *rows.shape[1:])[:, 0]
    paired = rows[1:].reshape(span_x // 2, 2, *rows.shape[1:])
    across = 0.25 * before + 0.5 * paired[:, 0] + 0.25 * paired[:, 1]
    cols = across[:, width_y - 2 * rim_y - 1:width_y + span_y + 2 * rim_y]
    count = span_y // 2 + 2 * rim_y
    before = cols[:, :-1].reshape(cols.shape[0], count, 2, cols.shape[2])[:, :, 0]
    paired = cols[:, 1:].reshape(cols.shape[0], count, 2, cols.shape[2])
    return 0.25 * before + 0.5 * paired[:, :, 0] + 0.25 * paired[:, :, 1]


def coarsen(values):
    paired = values.reshape(values.shape[0] // 2, 2, values.shape[1], values.shape[2])
    across = 0.5 * (paired[:, 0] + paired[:, 1])
    paired = across.reshape(across.shape[0], across.shape[1] // 2, 2, across.shape[2])
    return 0.5 * (paired[:, :, 0] + paired[:, :, 1])


def lift(coarse):
    return jnp.repeat(jnp.repeat(coarse, 2, axis=0), 2, axis=1)


def interior(values, width):
    return values[width:values.shape[0] - width, width:values.shape[1] - width]


def descend(grid_level, source, coefficient, width, width_y, rim_y):
    span_x, span_y = source.shape[0], source.shape[1]
    exchanger = lambda block, rim: along(along(block, width, "gx", 0), width_y, "gy", 1)
    source, coefficient_ext = exchange_many([source, coefficient], width, exchanger)
    weight = 0.25**grid_level
    divisor = 4.0 * weight + 2.0 + coefficient_ext
    allowed = inside(span_x, span_y, width, width_y=width_y)
    iterate = sweeps(jnp.zeros_like(source), source, divisor, weight, allowed, 1)
    residual = residual_of(iterate, source, divisor, weight, allowed)
    coarse_source = restrict(residual, width, width_y, span_x, span_y, rim_y)
    low = width_y - 2 * rim_y
    coarse_coefficient = coarsen(
        coefficient_ext[width:width + span_x, low:width_y + span_y + 2 * rim_y]
    )
    return iterate, source, divisor, weight, allowed, coarse_source, coarse_coefficient


def descend_whole_x(grid_level, source, coefficient, width):
    span_x, span_y = source.shape[0], source.shape[1] - 2 * width
    weight = 0.25**grid_level
    divisor = 4.0 * weight + 2.0 + coefficient
    allowed = inside(span_x, span_y, width, whole_x=True)
    iterate = sweeps(jnp.zeros_like(source), source, divisor, weight, allowed, 1)
    residual = residual_of(iterate, source, divisor, weight, allowed)
    residual = jnp.pad(residual, ((1, 0), (0, 0), (0, 0)))
    coarse_source = restrict(residual, 1, width, span_x, span_y)
    coarse_coefficient = coarsen(coefficient[:, width:width + span_y])
    return iterate, source, divisor, weight, allowed, coarse_source, coarse_coefficient


def coarsest_whole_x(source, coefficient, width):
    span_y = source.shape[1]
    exchanger = lambda block, rim: along(block, rim, "gy", 1)
    source, coefficient = exchange_many([source, coefficient], width, exchanger)
    span_x = source.shape[0]
    weight = 0.25**3
    divisor = 4.0 * weight + 2.0 + coefficient
    allowed = inside(span_x, span_y, width, whole_x=True)
    iterate = jnp.zeros_like(source)
    plan = [(0, 1, 0, 1, 0), (1, 0, 1)]
    for step, colours in enumerate(plan):
        if step > 0:
            iterate = exchanger(iterate[:, width:width + span_y], width)
        for colour in colours:
            iterate = half_sweep(iterate, source, divisor, weight, allowed, colour)
    cut = width - 2
    return iterate[:, cut:iterate.shape[1] - cut]


def x_window(values, start, length, margin):
    padded = jnp.pad(values, ((margin, margin), (0, 0), (0, 0)))
    return lax.dynamic_slice_in_dim(padded, start, length, axis=0)


def dirichlet_kernel(volts_ref, potential_ref, charge_ref, region_ref, packed_ref):
    region = region_ref[...]
    total = jnp.zeros(region.shape, jnp.float32)
    for electrode in range(volts_ref.shape[0]):
        total = total + jnp.where(region == electrode + 1, volts_ref[electrode], jnp.float32(0.0))
    depth = region.shape[2]
    packed_ref[:, :, 0:depth] = potential_ref[...]
    packed_ref[:, :, depth:2 * depth] = charge_ref[...]
    packed_ref[:, :, 2 * depth:3 * depth] = region.astype(jnp.float32)
    packed_ref[:, :, 3 * depth:4 * depth] = total


def packed_inputs(potential, charge, region, electrode_volts):
    span_x, span_y, depth = potential.shape
    vmem = pl.BlockSpec(memory_space=pltpu.VMEM)
    return pl.pallas_call(
        dirichlet_kernel,
        out_shape=jax.ShapeDtypeStruct((span_x, span_y, 4 * depth), jnp.float32),
        in_specs=[pl.BlockSpec(memory_space=pltpu.SMEM), vmem, vmem, vmem],
        out_specs=vmem,
    )(electrode_volts, potential, charge, region)


def body(potential, charge, region, electrode_volts):
    span_x, span_y, depth = potential.shape
    width = HALO_FINE
    packed = exchange(packed_inputs(potential, charge, region, electrode_volts), width)
    potential, charge, region_f, dirichlet = [
        packed[:, :, i * depth:(i + 1) * depth] for i in range(4)
    ]
    movable = jnp.logical_and(region_f == 0.0, inside(span_x, span_y, width))
    flat_sum, vertical = neighbour_sums(pad_plane(potential))
    source = (
        charge - (6.0 * potential - (flat_sum + vertical)) - screen * (jnp.exp(potential) - 1.0)
    )
    coefficient = screen * jnp.exp(potential)
    divisor = 4.0 * 1.0 + 2.0 + coefficient
    iterate = sweeps(dirichlet, source, divisor, 1.0, movable, 1)
    residual = residual_of(iterate, source, divisor, 1.0, movable)
    source_1 = restrict(residual, width, width, span_x, span_y)
    coefficient_1 = coarsen(interior(coefficient, width))

    level_1 = descend(1, source_1, coefficient_1, HALO_MID, HALO_1_Y, HALO_MID)
    source_2, coefficient_2 = level_1[5], level_1[6]
    span_x2 = source_2.shape[0]
    whole = gather_x(jnp.concatenate([source_2, coefficient_2], axis=2))
    level_2 = descend_whole_x(2, whole[:, :, :depth], whole[:, :, depth:], HALO_MID)
    iterate_3 = coarsest_whole_x(level_2[5], level_2[6], HALO_COARSE)

    iterate_2, source_2, divisor_2, weight_2, allowed_2 = level_2[:5]
    iterate_2 = sweeps(iterate_2 + lift(iterate_3), source_2, divisor_2, weight_2, allowed_2, 1)
    rim = HALO_MID // 2
    iterate_2 = exchange_y(iterate_2[:, HALO_MID:HALO_MID + source_2.shape[1] - 2 * HALO_MID], rim)
    iterate_2 = x_window(iterate_2, lax.axis_index("gx") * span_x2, span_x2 + 2 * rim, rim)

    cut = HALO_1_Y - HALO_MID
    iterate_1, source_1, divisor_1, allowed_1 = [
        values[:, cut:values.shape[1] - cut] for values in (level_1[0], level_1[1], level_1[2], level_1[4])
    ]
    weight_1 = level_1[3]
    iterate_1 = sweeps(iterate_1 + lift(iterate_2), source_1, divisor_1, weight_1, allowed_1, 1)
    lifted = lift(interior(iterate_1, HALO_MID // 2))

    iterate = iterate + jnp.where(movable, lifted, 0.0)
    iterate = sweeps(iterate, source, divisor, 1.0, movable, 1)
    return interior(iterate, width)


def solution(mesh):
    placed = (P("gx", "gy", None), P("gx", "gy", None), P("gx", "gy", None), P())
    return jax.shard_map(
        body, mesh=mesh, in_specs=placed, out_specs=P("gx", "gy", None), check_vma=False
    )
```

```python
import jax
import jax.numpy as jnp
from jax import lax
from jax.experimental import pallas as pl
from jax.experimental.pallas import tpu as pltpu
from jax.sharding import PartitionSpec as P

screen = 0.5

HALO_FINE = 4
HALO_MID = 4
HALO_COARSE = 4


def shifted(block, axis, distance):
    count = lax.axis_size(axis)
    route = [(i, i + distance) for i in range(count) if 0 <= i + distance < count]
    if not route:
        return jnp.zeros_like(block)
    return lax.ppermute(block, axis, route)


def exchange(block, width):
    block = jnp.concatenate(
        [shifted(block[-width:], "gx", 1), block, shifted(block[:width], "gx", -1)], axis=0
    )
    return jnp.concatenate(
        [shifted(block[:, -width:], "gy", 1), block, shifted(block[:, :width], "gy", -1)], axis=1
    )


def along(block, width, axis, dim):
    span = block.shape[dim]
    reach = -(-width // span)
    part = width - (reach - 1) * span
    low = [shifted(lax.slice_in_dim(block, span - part, span, axis=dim), axis, reach)]
    low += [shifted(block, axis, d) for d in range(reach - 1, 0, -1)]
    high = [shifted(block, axis, -d) for d in range(1, reach)]
    high += [shifted(lax.slice_in_dim(block, 0, part, axis=dim), axis, -reach)]
    return jnp.concatenate(low + [block] + high, axis=dim)


def exchange_y(block, width):
    return jnp.concatenate(
        [shifted(block[:, -width:], "gy", 1), block, shifted(block[:, :width], "gy", -1)], axis=1
    )


def gather_x(block):
    count, index = lax.axis_size("gx"), lax.axis_index("gx")
    group = 1
    while group < count:
        size = min(4, count // group)
        received = [block] + [
            lax.ppermute(block, "gx", [(i, i ^ (m * group)) for i in range(count)])
            for m in range(1, size)
        ]
        stacked = jnp.stack(received)
        own = (index // group) % size
        block = jnp.concatenate(
            [lax.dynamic_index_in_dim(stacked, q ^ own, keepdims=False) for q in range(size)], axis=0
        )
        group *= size
    return block


def exchange_many(arrays, width, exchanger=exchange):
    depth = arrays[0].shape[2]
    packed = exchanger(jnp.concatenate(arrays, axis=2), width)
    return [packed[:, :, i * depth:(i + 1) * depth] for i in range(len(arrays))]


def inside(span_x, span_y, width, whole_x=False):
    index_y = lax.axis_index("gy") * span_y - width + jnp.arange(span_y + 2 * width)
    total_y = span_y * lax.axis_size("gy")
    keep_y = (index_y >= 0) & (index_y < total_y)
    if whole_x:
        return jnp.broadcast_to(keep_y[None, :, None], (span_x, span_y + 2 * width, 1))
    index_x = lax.axis_index("gx") * span_x - width + jnp.arange(span_x + 2 * width)
    total_x = span_x * lax.axis_size("gx")
    keep_x = (index_x >= 0) & (index_x < total_x)
    return (keep_x[:, None] & keep_y[None, :])[:, :, None]


def pad_plane(values):
    return jnp.pad(values, ((1, 1), (1, 1), (0, 0)))


def neighbour_sums(padded):
    interior = padded[1:-1, 1:-1]
    flat_sum = padded[2:, 1:-1] + padded[:-2, 1:-1] + padded[1:-1, 2:] + padded[1:-1, :-2]
    padded_z = jnp.pad(interior, ((0, 0), (0, 0), (1, 1)))
    vertical = padded_z[:, :, 2:] + padded_z[:, :, :-2]
    return (flat_sum, vertical)


def checker(span_x, span_y, span_z):
    index_x = jnp.arange(span_x, dtype=jnp.int32)[:, None, None]
    index_y = jnp.arange(span_y, dtype=jnp.int32)[None, :, None]
    index_z = jnp.arange(span_z, dtype=jnp.int32)[None, None, :]
    return (index_x + index_y + index_z) % 2


def half_sweep(iterate, source, divisor, weight, allowed, colour):
    flat_sum, vertical = neighbour_sums(pad_plane(iterate))
    renewed = (source + weight * flat_sum + vertical) / divisor
    span_x, span_y, span_z = iterate.shape
    update = jnp.logical_and(checker(span_x, span_y, span_z) == colour, allowed)
    return jnp.where(update, renewed, iterate)


def sweeps(iterate, source, divisor, weight, allowed, count):
    for _ in range(count):
        iterate = half_sweep(iterate, source, divisor, weight, allowed, 0)
        iterate = half_sweep(iterate, source, divisor, weight, allowed, 1)
    return iterate


def residual_of(iterate, source, divisor, weight, allowed):
    flat_sum, vertical = neighbour_sums(pad_plane(iterate))
    residual = source - (divisor * iterate - (weight * flat_sum + vertical))
    return jnp.where(allowed, residual, 0.0)


def restrict(values, width_x, width_y, span_x, span_y):
    rows = values[width_x - 1:width_x + span_x]
    across = 0.25 * rows[0:-1:2] + 0.5 * rows[1::2] + 0.25 * rows[2::2]
    cols = across[:, width_y - 1:width_y + span_y]
    return 0.25 * cols[:, 0:-1:2] + 0.5 * cols[:, 1::2] + 0.25 * cols[:, 2::2]


def coarsen(values):
    across = 0.5 * (values[0::2] + values[1::2])
    return 0.5 * (across[:, 0::2] + across[:, 1::2])


def lift(coarse):
    return jnp.repeat(jnp.repeat(coarse, 2, axis=0), 2, axis=1)


def interior(values, width):
    return values[width:values.shape[0] - width, width:values.shape[1] - width]


def descend(grid_level, source, coefficient, width):
    span_x, span_y = source.shape[0], source.shape[1]
    source, coefficient_ext = exchange_many([source, coefficient], width)
    weight = 0.25**grid_level
    divisor = 4.0 * weight + 2.0 + coefficient_ext
    allowed = inside(span_x, span_y, width)
    iterate = sweeps(jnp.zeros_like(source), source, divisor, weight, allowed, 1)
    residual = residual_of(iterate, source, divisor, weight, allowed)
    coarse_source = restrict(residual, width, width, span_x, span_y)
    coarse_coefficient = coarsen(interior(coefficient_ext, width))
    return iterate, source, divisor, weight, allowed, coarse_source, coarse_coefficient


def descend_whole_x(grid_level, source, coefficient, width):
    span_y = source.shape[1]
    source, coefficient = exchange_many([source, coefficient], width, exchange_y)
    span_x = source.shape[0]
    weight = 0.25**grid_level
    divisor = 4.0 * weight + 2.0 + coefficient
    allowed = inside(span_x, span_y, width, whole_x=True)
    iterate = sweeps(jnp.zeros_like(source), source, divisor, weight, allowed, 1)
    residual = residual_of(iterate, source, divisor, weight, allowed)
    residual = jnp.pad(residual, ((1, 0), (0, 0), (0, 0)))
    coarse_source = restrict(residual, 1, width, span_x, span_y)
    coarse_coefficient = coarsen(coefficient[:, width:width + span_y])
    return iterate, source, divisor, weight, allowed, coarse_source, coarse_coefficient


def coarsest_whole_x(source, coefficient, width):
    span_y = source.shape[1]
    exchanger = lambda block, rim: along(block, rim, "gy", 1)
    source, coefficient = exchange_many([source, coefficient], width, exchanger)
    span_x = source.shape[0]
    weight = 0.25**3
    divisor = 4.0 * weight + 2.0 + coefficient
    allowed = inside(span_x, span_y, width, whole_x=True)
    iterate = jnp.zeros_like(source)
    plan = [(0, 1, 0, 1, 0), (1, 0, 1)]
    for step, colours in enumerate(plan):
        if step > 0:
            iterate = exchanger(iterate[:, width:width + span_y], width)
        for colour in colours:
            iterate = half_sweep(iterate, source, divisor, weight, allowed, colour)
    cut = width - 2
    return iterate[:, cut:iterate.shape[1] - cut]


def x_window(values, start, length, margin):
    padded = jnp.pad(values, ((margin, margin), (0, 0), (0, 0)))
    return lax.dynamic_slice_in_dim(padded, start, length, axis=0)


def dirichlet_kernel(volts_ref, potential_ref, charge_ref, region_ref, packed_ref):
    region = region_ref[...]
    total = jnp.zeros(region.shape, jnp.float32)
    for electrode in range(volts_ref.shape[0]):
        total = total + jnp.where(region == electrode + 1, volts_ref[electrode], jnp.float32(0.0))
    depth = region.shape[2]
    packed_ref[:, :, 0:depth] = potential_ref[...]
    packed_ref[:, :, depth:2 * depth] = charge_ref[...]
    packed_ref[:, :, 2 * depth:3 * depth] = region.astype(jnp.float32)
    packed_ref[:, :, 3 * depth:4 * depth] = total


def packed_inputs(potential, charge, region, electrode_volts):
    span_x, span_y, depth = potential.shape
    vmem = pl.BlockSpec(memory_space=pltpu.VMEM)
    return pl.pallas_call(
        dirichlet_kernel,
        out_shape=jax.ShapeDtypeStruct((span_x, span_y, 4 * depth), jnp.float32),
        in_specs=[pl.BlockSpec(memory_space=pltpu.SMEM), vmem, vmem, vmem],
        out_specs=vmem,
    )(electrode_volts, potential, charge, region)


def body(potential, charge, region, electrode_volts):
    span_x, span_y, depth = potential.shape
    width = HALO_FINE
    packed = exchange(packed_inputs(potential, charge, region, electrode_volts), width)
    potential, charge, region_f, dirichlet = [
        packed[:, :, i * depth:(i + 1) * depth] for i in range(4)
    ]
    movable = jnp.logical_and(region_f == 0.0, inside(span_x, span_y, width))
    flat_sum, vertical = neighbour_sums(pad_plane(potential))
    source = (
        charge - (6.0 * potential - (flat_sum + vertical)) - screen * (jnp.exp(potential) - 1.0)
    )
    coefficient = screen * jnp.exp(potential)
    divisor = 4.0 * 1.0 + 2.0 + coefficient
    iterate = sweeps(dirichlet, source, divisor, 1.0, movable, 1)
    residual = residual_of(iterate, source, divisor, 1.0, movable)
    source_1 = restrict(residual, width, width, span_x, span_y)
    coefficient_1 = coarsen(interior(coefficient, width))

    level_1 = descend(1, source_1, coefficient_1, HALO_MID)
    source_2, coefficient_2 = level_1[5], level_1[6]
    span_x2 = source_2.shape[0]
    whole = gather_x(jnp.concatenate([source_2, coefficient_2], axis=2))
    level_2 = descend_whole_x(2, whole[:, :, :depth], whole[:, :, depth:], HALO_MID)
    iterate_3 = coarsest_whole_x(level_2[5], level_2[6], HALO_COARSE)

    iterate_2, source_2, divisor_2, weight_2, allowed_2 = level_2[:5]
    iterate_2 = sweeps(iterate_2 + lift(iterate_3), source_2, divisor_2, weight_2, allowed_2, 1)
    rim = HALO_MID // 2
    iterate_2 = exchange_y(iterate_2[:, HALO_MID:HALO_MID + source_2.shape[1] - 2 * HALO_MID], rim)
    iterate_2 = x_window(iterate_2, lax.axis_index("gx") * span_x2, span_x2 + 2 * rim, rim)

    iterate_1, source_1, divisor_1, weight_1, allowed_1 = level_1[:5]
    iterate_1 = sweeps(iterate_1 + lift(iterate_2), source_1, divisor_1, weight_1, allowed_1, 1)
    lifted = lift(interior(iterate_1, HALO_MID // 2))

    iterate = iterate + jnp.where(movable, lifted, 0.0)
    iterate = sweeps(iterate, source, divisor, 1.0, movable, 1)
    return interior(iterate, width)


def solution(mesh):
    placed = (P("gx", "gy", None), P("gx", "gy", None), P("gx", "gy", None), P())
    return jax.shard_map(
        body, mesh=mesh, in_specs=placed, out_specs=P("gx", "gy", None), check_vma=False
    )
```

```python
import jax
import jax.numpy as jnp
from jax import lax
from jax.experimental import pallas as pl
from jax.experimental.pallas import tpu as pltpu
from jax.sharding import PartitionSpec as P

screen = 0.5

HALO_FINE = 4
HALO_MID = 4
HALO_COARSE = 4


def shifted(block, axis, distance):
    count = lax.axis_size(axis)
    route = [(i, i + distance) for i in range(count) if 0 <= i + distance < count]
    if not route:
        return jnp.zeros_like(block)
    return lax.ppermute(block, axis, route)


def exchange(block, width):
    block = jnp.concatenate(
        [shifted(block[-width:], "gx", 1), block, shifted(block[:width], "gx", -1)], axis=0
    )
    return jnp.concatenate(
        [shifted(block[:, -width:], "gy", 1), block, shifted(block[:, :width], "gy", -1)], axis=1
    )


def along(block, width, axis, dim):
    span = block.shape[dim]
    reach = -(-width // span)
    part = width - (reach - 1) * span
    low = [shifted(lax.slice_in_dim(block, span - part, span, axis=dim), axis, reach)]
    low += [shifted(block, axis, d) for d in range(reach - 1, 0, -1)]
    high = [shifted(block, axis, -d) for d in range(1, reach)]
    high += [shifted(lax.slice_in_dim(block, 0, part, axis=dim), axis, -reach)]
    return jnp.concatenate(low + [block] + high, axis=dim)


def exchange_y(block, width):
    return jnp.concatenate(
        [shifted(block[:, -width:], "gy", 1), block, shifted(block[:, :width], "gy", -1)], axis=1
    )


def gather_x(block):
    count, index = lax.axis_size("gx"), lax.axis_index("gx")
    group = 1
    while group < count:
        size = min(4, count // group)
        received = [block] + [
            lax.ppermute(block, "gx", [(i, i ^ (m * group)) for i in range(count)])
            for m in range(1, size)
        ]
        stacked = jnp.stack(received)
        own = (index // group) % size
        block = jnp.concatenate(
            [lax.dynamic_index_in_dim(stacked, q ^ own, keepdims=False) for q in range(size)], axis=0
        )
        group *= size
    return block


def exchange_many(arrays, width, exchanger=exchange):
    depth = arrays[0].shape[2]
    packed = exchanger(jnp.concatenate(arrays, axis=2), width)
    return [packed[:, :, i * depth:(i + 1) * depth] for i in range(len(arrays))]


def inside(span_x, span_y, width, whole_x=False):
    index_y = lax.axis_index("gy") * span_y - width + jnp.arange(span_y + 2 * width)
    total_y = span_y * lax.axis_size("gy")
    keep_y = (index_y >= 0) & (index_y < total_y)
    if whole_x:
        return jnp.broadcast_to(keep_y[None, :, None], (span_x, span_y + 2 * width, 1))
    index_x = lax.axis_index("gx") * span_x - width + jnp.arange(span_x + 2 * width)
    total_x = span_x * lax.axis_size("gx")
    keep_x = (index_x >= 0) & (index_x < total_x)
    return (keep_x[:, None] & keep_y[None, :])[:, :, None]


def pad_plane(values):
    return jnp.pad(values, ((1, 1), (1, 1), (0, 0)))


def neighbour_sums(padded):
    interior = padded[1:-1, 1:-1]
    flat_sum = padded[2:, 1:-1] + padded[:-2, 1:-1] + padded[1:-1, 2:] + padded[1:-1, :-2]
    padded_z = jnp.pad(interior, ((0, 0), (0, 0), (1, 1)))
    vertical = padded_z[:, :, 2:] + padded_z[:, :, :-2]
    return (flat_sum, vertical)


def checker(span_x, span_y, span_z):
    index_x = jnp.arange(span_x, dtype=jnp.int32)[:, None, None]
    index_y = jnp.arange(span_y, dtype=jnp.int32)[None, :, None]
    index_z = jnp.arange(span_z, dtype=jnp.int32)[None, None, :]
    return (index_x + index_y + index_z) % 2


def half_sweep(iterate, source, divisor, weight, allowed, colour):
    flat_sum, vertical = neighbour_sums(pad_plane(iterate))
    renewed = (source + weight * flat_sum + vertical) / divisor
    span_x, span_y, span_z = iterate.shape
    update = jnp.logical_and(checker(span_x, span_y, span_z) == colour, allowed)
    return jnp.where(update, renewed, iterate)


def sweeps(iterate, source, divisor, weight, allowed, count):
    for _ in range(count):
        iterate = half_sweep(iterate, source, divisor, weight, allowed, 0)
        iterate = half_sweep(iterate, source, divisor, weight, allowed, 1)
    return iterate


def residual_of(iterate, source, divisor, weight, allowed):
    flat_sum, vertical = neighbour_sums(pad_plane(iterate))
    residual = source - (divisor * iterate - (weight * flat_sum + vertical))
    return jnp.where(allowed, residual, 0.0)


def restrict(values, width_x, width_y, span_x, span_y):
    rows = values[width_x - 1:width_x + span_x, width_y - 1:width_y + span_y]
    cols = 0.25 * rows[0:-1:2] + 0.5 * rows[1::2] + 0.25 * rows[2::2]
    return 0.25 * cols[:, 0:-1:2] + 0.5 * cols[:, 1::2] + 0.25 * cols[:, 2::2]


def coarsen(values):
    across = 0.5 * (values[0::2] + values[1::2])
    return 0.5 * (across[:, 0::2] + across[:, 1::2])


def lift(coarse):
    return jnp.repeat(jnp.repeat(coarse, 2, axis=0), 2, axis=1)


def interior(values, width):
    return values[width:values.shape[0] - width, width:values.shape[1] - width]


def descend(grid_level, source, coefficient, width):
    span_x, span_y = source.shape[0], source.shape[1]
    source, coefficient_ext = exchange_many([source, coefficient], width)
    weight = 0.25**grid_level
    divisor = 4.0 * weight + 2.0 + coefficient_ext
    allowed = inside(span_x, span_y, width)
    iterate = sweeps(jnp.zeros_like(source), source, divisor, weight, allowed, 1)
    residual = residual_of(iterate, source, divisor, weight, allowed)
    coarse_source = restrict(residual, width, width, span_x, span_y)
    coarse_coefficient = coarsen(interior(coefficient_ext, width))
    return iterate, source, divisor, weight, allowed, coarse_source, coarse_coefficient


def descend_whole_x(grid_level, source, coefficient, width):
    span_y = source.shape[1]
    source, coefficient = exchange_many([source, coefficient], width, exchange_y)
    span_x = source.shape[0]
    weight = 0.25**grid_level
    divisor = 4.0 * weight + 2.0 + coefficient
    allowed = inside(span_x, span_y, width, whole_x=True)
    iterate = sweeps(jnp.zeros_like(source), source, divisor, weight, allowed, 1)
    residual = residual_of(iterate, source, divisor, weight, allowed)
    residual = jnp.pad(residual, ((1, 0), (0, 0), (0, 0)))
    coarse_source = restrict(residual, 1, width, span_x, span_y)
    coarse_coefficient = coarsen(coefficient[:, width:width + span_y])
    return iterate, source, divisor, weight, allowed, coarse_source, coarse_coefficient


def coarsest_whole_x(source, coefficient, width):
    span_y = source.shape[1]
    exchanger = lambda block, rim: along(block, rim, "gy", 1)
    source, coefficient = exchange_many([source, coefficient], width, exchanger)
    span_x = source.shape[0]
    weight = 0.25**3
    divisor = 4.0 * weight + 2.0 + coefficient
    allowed = inside(span_x, span_y, width, whole_x=True)
    iterate = jnp.zeros_like(source)
    plan = [(0, 1, 0, 1, 0), (1, 0, 1)]
    for step, colours in enumerate(plan):
        if step > 0:
            iterate = exchanger(iterate[:, width:width + span_y], width)
        for colour in colours:
            iterate = half_sweep(iterate, source, divisor, weight, allowed, colour)
    cut = width - 2
    return iterate[:, cut:iterate.shape[1] - cut]


def x_window(values, start, length, margin):
    padded = jnp.pad(values, ((margin, margin), (0, 0), (0, 0)))
    return lax.dynamic_slice_in_dim(padded, start, length, axis=0)


def dirichlet_kernel(volts_ref, potential_ref, charge_ref, region_ref, packed_ref):
    region = region_ref[...]
    total = jnp.zeros(region.shape, jnp.float32)
    for electrode in range(volts_ref.shape[0]):
        total = total + jnp.where(region == electrode + 1, volts_ref[electrode], jnp.float32(0.0))
    depth = region.shape[2]
    packed_ref[:, :, 0:depth] = potential_ref[...]
    packed_ref[:, :, depth:2 * depth] = charge_ref[...]
    packed_ref[:, :, 2 * depth:3 * depth] = region.astype(jnp.float32)
    packed_ref[:, :, 3 * depth:4 * depth] = total


def packed_inputs(potential, charge, region, electrode_volts):
    span_x, span_y, depth = potential.shape
    vmem = pl.BlockSpec(memory_space=pltpu.VMEM)
    return pl.pallas_call(
        dirichlet_kernel,
        out_shape=jax.ShapeDtypeStruct((span_x, span_y, 4 * depth), jnp.float32),
        in_specs=[pl.BlockSpec(memory_space=pltpu.SMEM), vmem, vmem, vmem],
        out_specs=vmem,
    )(electrode_volts, potential, charge, region)


def body(potential, charge, region, electrode_volts):
    span_x, span_y, depth = potential.shape
    width = HALO_FINE
    packed = exchange(packed_inputs(potential, charge, region, electrode_volts), width)
    potential, charge, region_f, dirichlet = [
        packed[:, :, i * depth:(i + 1) * depth] for i in range(4)
    ]
    movable = jnp.logical_and(region_f == 0.0, inside(span_x, span_y, width))
    flat_sum, vertical = neighbour_sums(pad_plane(potential))
    source = (
        charge - (6.0 * potential - (flat_sum + vertical)) - screen * (jnp.exp(potential) - 1.0)
    )
    coefficient = screen * jnp.exp(potential)
    divisor = 4.0 * 1.0 + 2.0 + coefficient
    iterate = sweeps(dirichlet, source, divisor, 1.0, movable, 1)
    residual = residual_of(iterate, source, divisor, 1.0, movable)
    source_1 = restrict(residual, width, width, span_x, span_y)
    coefficient_1 = coarsen(interior(coefficient, width))

    level_1 = descend(1, source_1, coefficient_1, HALO_MID)
    source_2, coefficient_2 = level_1[5], level_1[6]
    span_x2 = source_2.shape[0]
    whole = gather_x(jnp.concatenate([source_2, coefficient_2], axis=2))
    level_2 = descend_whole_x(2, whole[:, :, :depth], whole[:, :, depth:], HALO_MID)
    iterate_3 = coarsest_whole_x(level_2[5], level_2[6], HALO_COARSE)

    iterate_2, source_2, divisor_2, weight_2, allowed_2 = level_2[:5]
    iterate_2 = sweeps(iterate_2 + lift(iterate_3), source_2, divisor_2, weight_2, allowed_2, 1)
    rim = HALO_MID // 2
    iterate_2 = exchange_y(iterate_2[:, HALO_MID:HALO_MID + source_2.shape[1] - 2 * HALO_MID], rim)
    iterate_2 = x_window(iterate_2, lax.axis_index("gx") * span_x2, span_x2 + 2 * rim, rim)

    iterate_1, source_1, divisor_1, weight_1, allowed_1 = level_1[:5]
    iterate_1 = sweeps(iterate_1 + lift(iterate_2), source_1, divisor_1, weight_1, allowed_1, 1)
    lifted = lift(interior(iterate_1, HALO_MID // 2))

    iterate = iterate + jnp.where(movable, lifted, 0.0)
    iterate = sweeps(iterate, source, divisor, 1.0, movable, 1)
    return interior(iterate, width)


def solution(mesh):
    placed = (P("gx", "gy", None), P("gx", "gy", None), P("gx", "gy", None), P())
    return jax.shard_map(
        body, mesh=mesh, in_specs=placed, out_specs=P("gx", "gy", None), check_vma=False
    )
```

```python
import jax
import jax.numpy as jnp
from jax import lax
from jax.experimental import pallas as pl
from jax.experimental.pallas import tpu as pltpu
from jax.sharding import PartitionSpec as P

screen = 0.5

HALO_FINE = 4
HALO_MID = 4
HALO_COARSE = 4


def shifted(block, axis, distance):
    count = lax.axis_size(axis)
    route = [(i, i + distance) for i in range(count) if 0 <= i + distance < count]
    if not route:
        return jnp.zeros_like(block)
    return lax.ppermute(block, axis, route)


def exchange(block, width):
    block = jnp.concatenate(
        [shifted(block[-width:], "gx", 1), block, shifted(block[:width], "gx", -1)], axis=0
    )
    return jnp.concatenate(
        [shifted(block[:, -width:], "gy", 1), block, shifted(block[:, :width], "gy", -1)], axis=1
    )


def along(block, width, axis, dim):
    span = block.shape[dim]
    reach = -(-width // span)
    part = width - (reach - 1) * span
    low = [shifted(lax.slice_in_dim(block, span - part, span, axis=dim), axis, reach)]
    low += [shifted(block, axis, d) for d in range(reach - 1, 0, -1)]
    high = [shifted(block, axis, -d) for d in range(1, reach)]
    high += [shifted(lax.slice_in_dim(block, 0, part, axis=dim), axis, -reach)]
    return jnp.concatenate(low + [block] + high, axis=dim)


def exchange_y(block, width):
    return jnp.concatenate(
        [shifted(block[:, -width:], "gy", 1), block, shifted(block[:, :width], "gy", -1)], axis=1
    )


def gather_x(block):
    count, index = lax.axis_size("gx"), lax.axis_index("gx")
    group = 1
    while group < count:
        size = min(4, count // group)
        received = [block] + [
            lax.ppermute(block, "gx", [(i, i ^ (m * group)) for i in range(count)])
            for m in range(1, size)
        ]
        stacked = jnp.stack(received)
        own = (index // group) % size
        block = jnp.concatenate(
            [lax.dynamic_index_in_dim(stacked, q ^ own, keepdims=False) for q in range(size)], axis=0
        )
        group *= size
    return block


def exchange_many(arrays, width, exchanger=exchange):
    depth = arrays[0].shape[2]
    packed = exchanger(jnp.concatenate(arrays, axis=2), width)
    return [packed[:, :, i * depth:(i + 1) * depth] for i in range(len(arrays))]


def inside(span_x, span_y, width, whole_x=False):
    index_y = lax.axis_index("gy") * span_y - width + jnp.arange(span_y + 2 * width)
    total_y = span_y * lax.axis_size("gy")
    keep_y = (index_y >= 0) & (index_y < total_y)
    if whole_x:
        return jnp.broadcast_to(keep_y[None, :, None], (span_x, span_y + 2 * width, 1))
    index_x = lax.axis_index("gx") * span_x - width + jnp.arange(span_x + 2 * width)
    total_x = span_x * lax.axis_size("gx")
    keep_x = (index_x >= 0) & (index_x < total_x)
    return (keep_x[:, None] & keep_y[None, :])[:, :, None]


def pad_plane(values):
    return jnp.pad(values, ((1, 1), (1, 1), (0, 0)))


def neighbour_sums(padded):
    interior = padded[1:-1, 1:-1]
    flat_sum = padded[2:, 1:-1] + padded[:-2, 1:-1] + padded[1:-1, 2:] + padded[1:-1, :-2]
    padded_z = jnp.pad(interior, ((0, 0), (0, 0), (1, 1)))
    vertical = padded_z[:, :, 2:] + padded_z[:, :, :-2]
    return (flat_sum, vertical)


def checker(span_x, span_y, span_z):
    index_x = jnp.arange(span_x, dtype=jnp.int32)[:, None, None]
    index_y = jnp.arange(span_y, dtype=jnp.int32)[None, :, None]
    index_z = jnp.arange(span_z, dtype=jnp.int32)[None, None, :]
    return (index_x + index_y + index_z) % 2


def half_sweep(iterate, source, divisor, weight, allowed, colour):
    flat_sum, vertical = neighbour_sums(pad_plane(iterate))
    renewed = (source + weight * flat_sum + vertical) / divisor
    span_x, span_y, span_z = iterate.shape
    update = jnp.logical_and(checker(span_x, span_y, span_z) == colour, allowed)
    return jnp.where(update, renewed, iterate)


def sweeps(iterate, source, divisor, weight, allowed, count):
    for _ in range(count):
        iterate = half_sweep(iterate, source, divisor, weight, allowed, 0)
        iterate = half_sweep(iterate, source, divisor, weight, allowed, 1)
    return iterate


def residual_of(iterate, source, divisor, weight, allowed):
    flat_sum, vertical = neighbour_sums(pad_plane(iterate))
    residual = source - (divisor * iterate - (weight * flat_sum + vertical))
    return jnp.where(allowed, residual, 0.0)


def restrict(values, width_x, width_y, span_x, span_y):
    rows = values[width_x - 1:width_x + span_x, width_y - 1:width_y + span_y]
    cols = 0.25 * rows[0:-1:2] + 0.5 * rows[1::2] + 0.25 * rows[2::2]
    return 0.25 * cols[:, 0:-1:2] + 0.5 * cols[:, 1::2] + 0.25 * cols[:, 2::2]


def coarsen(values):
    across = 0.5 * (values[0::2] + values[1::2])
    return 0.5 * (across[:, 0::2] + across[:, 1::2])


def lift(coarse):
    return jnp.repeat(jnp.repeat(coarse, 2, axis=0), 2, axis=1)


def interior(values, width):
    return values[width:values.shape[0] - width, width:values.shape[1] - width]


def descend(grid_level, source, coefficient, width):
    span_x, span_y = source.shape[0], source.shape[1]
    source, coefficient_ext = exchange_many([source, coefficient], width)
    weight = 0.25**grid_level
    divisor = 4.0 * weight + 2.0 + coefficient_ext
    allowed = inside(span_x, span_y, width)
    iterate = sweeps(jnp.zeros_like(source), source, divisor, weight, allowed, 1)
    residual = residual_of(iterate, source, divisor, weight, allowed)
    coarse_source = restrict(residual, width, width, span_x, span_y)
    coarse_coefficient = coarsen(interior(coefficient_ext, width))
    return iterate, source, divisor, weight, allowed, coarse_source, coarse_coefficient


def descend_whole_x(grid_level, source, coefficient, width):
    span_y = source.shape[1]
    source, coefficient = exchange_many([source, coefficient], width, exchange_y)
    span_x = source.shape[0]
    weight = 0.25**grid_level
    divisor = 4.0 * weight + 2.0 + coefficient
    allowed = inside(span_x, span_y, width, whole_x=True)
    iterate = sweeps(jnp.zeros_like(source), source, divisor, weight, allowed, 1)
    residual = residual_of(iterate, source, divisor, weight, allowed)
    residual = jnp.pad(residual, ((1, 0), (0, 0), (0, 0)))
    coarse_source = restrict(residual, 1, width, span_x, span_y)
    coarse_coefficient = coarsen(coefficient[:, width:width + span_y])
    return iterate, source, divisor, weight, allowed, coarse_source, coarse_coefficient


def coarsest_whole_x(source, coefficient, width):
    span_y = source.shape[1]
    exchanger = lambda block, rim: along(block, rim, "gy", 1)
    source, coefficient = exchange_many([source, coefficient], width, exchanger)
    span_x = source.shape[0]
    weight = 0.25**3
    divisor = 4.0 * weight + 2.0 + coefficient
    allowed = inside(span_x, span_y, width, whole_x=True)
    iterate = jnp.zeros_like(source)
    plan = [(0, 1, 0, 1, 0), (1, 0, 1)]
    for step, colours in enumerate(plan):
        if step > 0:
            iterate = exchanger(iterate[:, width:width + span_y], width)
        for colour in colours:
            iterate = half_sweep(iterate, source, divisor, weight, allowed, colour)
    cut = width - 2
    return iterate[:, cut:iterate.shape[1] - cut]


def x_window(values, start, length, margin):
    padded = jnp.pad(values, ((margin, margin), (0, 0), (0, 0)))
    return lax.dynamic_slice_in_dim(padded, start, length, axis=0)


def dirichlet_kernel(volts_ref, potential_ref, charge_ref, region_ref, packed_ref):
    region = region_ref[...]
    total = jnp.zeros(region.shape, jnp.float32)
    for electrode in range(volts_ref.shape[0]):
        total = total + jnp.where(region == electrode + 1, volts_ref[electrode], jnp.float32(0.0))
    depth = region.shape[2]
    packed_ref[:, :, 0:depth] = potential_ref[...]
    packed_ref[:, :, depth:2 * depth] = charge_ref[...]
    packed_ref[:, :, 2 * depth:3 * depth] = region.astype(jnp.float32)
    packed_ref[:, :, 3 * depth:4 * depth] = total


def packed_inputs(potential, charge, region, electrode_volts):
    span_x, span_y, depth = potential.shape
    vmem = pl.BlockSpec(memory_space=pltpu.VMEM)
    return pl.pallas_call(
        dirichlet_kernel,
        out_shape=jax.ShapeDtypeStruct((span_x, span_y, 4 * depth), jnp.float32),
        in_specs=[pl.BlockSpec(memory_space=pltpu.SMEM), vmem, vmem, vmem],
        out_specs=vmem,
    )(electrode_volts, potential, charge, region)


def body(potential, charge, region, electrode_volts):
    span_x, span_y, depth = potential.shape
    width = HALO_FINE
    packed = exchange(packed_inputs(potential, charge, region, electrode_volts), width)
    potential, charge, region_f, dirichlet = [
        packed[:, :, i * depth:(i + 1) * depth] for i in range(4)
    ]
    movable = jnp.logical_and(region_f == 0.0, inside(span_x, span_y, width))
    flat_sum, vertical = neighbour_sums(pad_plane(potential))
    source = (
        charge - (6.0 * potential - (flat_sum + vertical)) - screen * (jnp.exp(potential) - 1.0)
    )
    coefficient = screen * jnp.exp(potential)
    divisor = 4.0 * 1.0 + 2.0 + coefficient
    iterate = sweeps(dirichlet, source, divisor, 1.0, movable, 1)
    residual = residual_of(iterate, source, divisor, 1.0, movable)
    source_1 = restrict(residual, width, width, span_x, span_y)
    coefficient_1 = coarsen(interior(coefficient, width))

    level_1 = descend(1, source_1, coefficient_1, HALO_MID)
    source_2, coefficient_2 = level_1[5], level_1[6]
    span_x2 = source_2.shape[0]
    whole = gather_x(jnp.concatenate([source_2, coefficient_2], axis=2))
    level_2 = descend_whole_x(2, whole[:, :, :depth], whole[:, :, depth:], HALO_MID)
    iterate_3 = coarsest_whole_x(level_2[5], level_2[6], HALO_COARSE)

    iterate_2, source_2, divisor_2, weight_2, allowed_2 = level_2[:5]
    iterate_2 = sweeps(iterate_2 + lift(iterate_3), source_2, divisor_2, weight_2, allowed_2, 1)
    rim = HALO_MID // 2
    iterate_2 = exchange_y(iterate_2[:, HALO_MID:HALO_MID + source_2.shape[1] - 2 * HALO_MID], rim)
    iterate_2 = x_window(iterate_2, lax.axis_index("gx") * span_x2, span_x2 + 2 * rim, rim)

    iterate_1, source_1, divisor_1, weight_1, allowed_1 = level_1[:5]
    iterate_1 = sweeps(iterate_1 + lift(iterate_2), source_1, divisor_1, weight_1, allowed_1, 1)
    cut = width - 2
    lifted = lift(interior(iterate_1, HALO_MID - 1))
    movable = interior(movable, cut)
    iterate = interior(iterate, cut) + jnp.where(movable, lifted, 0.0)
    iterate = sweeps(iterate, interior(source, cut), interior(divisor, cut), 1.0, movable, 1)
    return interior(iterate, 2)


def solution(mesh):
    placed = (P("gx", "gy", None), P("gx", "gy", None), P("gx", "gy", None), P())
    return jax.shard_map(
        body, mesh=mesh, in_specs=placed, out_specs=P("gx", "gy", None), check_vma=False
    )
```

```python
import jax
import jax.numpy as jnp
from jax import lax
from jax.experimental import pallas as pl
from jax.experimental.pallas import tpu as pltpu
from jax.sharding import PartitionSpec as P

screen = 0.5

HALO_FINE = 4
HALO_MID = 4
HALO_COARSE = 4


def shifted(block, axis, distance):
    count = lax.axis_size(axis)
    route = [(i, i + distance) for i in range(count) if 0 <= i + distance < count]
    if not route:
        return jnp.zeros_like(block)
    return lax.ppermute(block, axis, route)


def exchange(block, width):
    block = jnp.concatenate(
        [shifted(block[-width:], "gx", 1), block, shifted(block[:width], "gx", -1)], axis=0
    )
    return jnp.concatenate(
        [shifted(block[:, -width:], "gy", 1), block, shifted(block[:, :width], "gy", -1)], axis=1
    )


def along(block, width, axis, dim):
    span = block.shape[dim]
    reach = -(-width // span)
    part = width - (reach - 1) * span
    low = [shifted(lax.slice_in_dim(block, span - part, span, axis=dim), axis, reach)]
    low += [shifted(block, axis, d) for d in range(reach - 1, 0, -1)]
    high = [shifted(block, axis, -d) for d in range(1, reach)]
    high += [shifted(lax.slice_in_dim(block, 0, part, axis=dim), axis, -reach)]
    return jnp.concatenate(low + [block] + high, axis=dim)


def exchange_y(block, width):
    return jnp.concatenate(
        [shifted(block[:, -width:], "gy", 1), block, shifted(block[:, :width], "gy", -1)], axis=1
    )


def gather_x(block):
    count, index = lax.axis_size("gx"), lax.axis_index("gx")
    group = 1
    while group < count:
        size = min(4, count // group)
        received = [block] + [
            lax.ppermute(block, "gx", [(i, i ^ (m * group)) for i in range(count)])
            for m in range(1, size)
        ]
        stacked = jnp.stack(received)
        own = (index // group) % size
        block = jnp.concatenate(
            [lax.dynamic_index_in_dim(stacked, q ^ own, keepdims=False) for q in range(size)], axis=0
        )
        group *= size
    return block


def exchange_many(arrays, width, exchanger=exchange):
    depth = arrays[0].shape[2]
    packed = exchanger(jnp.concatenate(arrays, axis=2), width)
    return [packed[:, :, i * depth:(i + 1) * depth] for i in range(len(arrays))]


def inside(span_x, span_y, width, whole_x=False):
    index_y = lax.axis_index("gy") * span_y - width + jnp.arange(span_y + 2 * width)
    total_y = span_y * lax.axis_size("gy")
    keep_y = (index_y >= 0) & (index_y < total_y)
    if whole_x:
        return jnp.broadcast_to(keep_y[None, :, None], (span_x, span_y + 2 * width, 1))
    index_x = lax.axis_index("gx") * span_x - width + jnp.arange(span_x + 2 * width)
    total_x = span_x * lax.axis_size("gx")
    keep_x = (index_x >= 0) & (index_x < total_x)
    return (keep_x[:, None] & keep_y[None, :])[:, :, None]


def pad_plane(values):
    return jnp.pad(values, ((1, 1), (1, 1), (0, 0)))


def neighbour_sums(padded):
    interior = padded[1:-1, 1:-1]
    flat_sum = padded[2:, 1:-1] + padded[:-2, 1:-1] + padded[1:-1, 2:] + padded[1:-1, :-2]
    padded_z = jnp.pad(interior, ((0, 0), (0, 0), (1, 1)))
    vertical = padded_z[:, :, 2:] + padded_z[:, :, :-2]
    return (flat_sum, vertical)


def checker(span_x, span_y, span_z):
    index_x = jnp.arange(span_x, dtype=jnp.int32)[:, None, None]
    index_y = jnp.arange(span_y, dtype=jnp.int32)[None, :, None]
    index_z = jnp.arange(span_z, dtype=jnp.int32)[None, None, :]
    return (index_x + index_y + index_z) % 2


def half_sweep(iterate, source, divisor, weight, allowed, colour):
    flat_sum, vertical = neighbour_sums(pad_plane(iterate))
    renewed = (source + weight * flat_sum + vertical) / divisor
    span_x, span_y, span_z = iterate.shape
    update = jnp.logical_and(checker(span_x, span_y, span_z) == colour, allowed)
    return jnp.where(update, renewed, iterate)


def sweeps(iterate, source, divisor, weight, allowed, count):
    for _ in range(count):
        iterate = half_sweep(iterate, source, divisor, weight, allowed, 0)
        iterate = half_sweep(iterate, source, divisor, weight, allowed, 1)
    return iterate


def residual_of(iterate, source, divisor, weight, allowed):
    flat_sum, vertical = neighbour_sums(pad_plane(iterate))
    residual = source - (divisor * iterate - (weight * flat_sum + vertical))
    return jnp.where(allowed, residual, 0.0)


def restrict(values, width_x, width_y, span_x, span_y):
    rows = values[width_x - 1:width_x + span_x, width_y - 1:width_y + span_y]
    cols = 0.25 * rows[0:-1:2] + 0.5 * rows[1::2] + 0.25 * rows[2::2]
    return 0.25 * cols[:, 0:-1:2] + 0.5 * cols[:, 1::2] + 0.25 * cols[:, 2::2]


def coarsen(values):
    across = 0.5 * (values[0::2] + values[1::2])
    return 0.5 * (across[:, 0::2] + across[:, 1::2])


def lift(coarse):
    return jnp.repeat(jnp.repeat(coarse, 2, axis=0), 2, axis=1)


def interior(values, width):
    return values[width:values.shape[0] - width, width:values.shape[1] - width]


def descend(grid_level, source, coefficient, width):
    span_x, span_y = source.shape[0], source.shape[1]
    source, coefficient_ext = exchange_many([source, coefficient], width)
    weight = 0.25**grid_level
    divisor = 4.0 * weight + 2.0 + coefficient_ext
    allowed = inside(span_x, span_y, width)
    iterate = sweeps(jnp.zeros_like(source), source, divisor, weight, allowed, 1)
    residual = residual_of(iterate, source, divisor, weight, allowed)
    coarse_source = restrict(residual, width, width, span_x, span_y)
    coarse_coefficient = coarsen(interior(coefficient_ext, width))
    return iterate, source, divisor, weight, allowed, coarse_source, coarse_coefficient


def descend_whole_x(grid_level, source, coefficient, width):
    span_y = source.shape[1]
    source, coefficient = exchange_many([source, coefficient], width, exchange_y)
    span_x = source.shape[0]
    weight = 0.25**grid_level
    divisor = 4.0 * weight + 2.0 + coefficient
    allowed = inside(span_x, span_y, width, whole_x=True)
    iterate = sweeps(jnp.zeros_like(source), source, divisor, weight, allowed, 1)
    residual = residual_of(iterate, source, divisor, weight, allowed)
    residual = jnp.pad(residual, ((1, 0), (0, 0), (0, 0)))
    coarse_source = restrict(residual, 1, width, span_x, span_y)
    coarse_coefficient = coarsen(coefficient[:, width:width + span_y])
    return iterate, source, divisor, weight, allowed, coarse_source, coarse_coefficient


def coarsest_whole_x(source, coefficient, width):
    span_y = source.shape[1]
    exchanger = lambda block, rim: along(block, rim, "gy", 1)
    source, coefficient = exchange_many([source, coefficient], width, exchanger)
    span_x = source.shape[0]
    weight = 0.25**3
    divisor = 4.0 * weight + 2.0 + coefficient
    allowed = inside(span_x, span_y, width, whole_x=True)
    iterate = jnp.zeros_like(source)
    plan = [(0, 1, 0, 1, 0), (1, 0, 1)]
    for step, colours in enumerate(plan):
        if step > 0:
            iterate = exchanger(iterate[:, width:width + span_y], width)
        for colour in colours:
            iterate = half_sweep(iterate, source, divisor, weight, allowed, colour)
    cut = width - 2
    return iterate[:, cut:iterate.shape[1] - cut]


def x_window(values, start, length, margin):
    padded = jnp.pad(values, ((margin, margin), (0, 0), (0, 0)))
    return lax.dynamic_slice_in_dim(padded, start, length, axis=0)


def dirichlet_kernel(volts_ref, potential_ref, charge_ref, region_ref, packed_ref):
    region = region_ref[...]
    total = jnp.zeros(region.shape, jnp.float32)
    for electrode in range(volts_ref.shape[0]):
        total = total + jnp.where(region == electrode + 1, volts_ref[electrode], jnp.float32(0.0))
    depth = region.shape[2]
    packed_ref[:, :, 0:depth] = potential_ref[...]
    packed_ref[:, :, depth:2 * depth] = charge_ref[...]
    packed_ref[:, :, 2 * depth:3 * depth] = region.astype(jnp.float32)
    packed_ref[:, :, 3 * depth:4 * depth] = total


def packed_inputs(potential, charge, region, electrode_volts):
    span_x, span_y, depth = potential.shape
    vmem = pl.BlockSpec(memory_space=pltpu.VMEM)
    return pl.pallas_call(
        dirichlet_kernel,
        out_shape=jax.ShapeDtypeStruct((span_x, span_y, 4 * depth), jnp.float32),
        in_specs=[pl.BlockSpec(memory_space=pltpu.SMEM), vmem, vmem, vmem],
        out_specs=vmem,
    )(electrode_volts, potential, charge, region)


def body(potential, charge, region, electrode_volts):
    span_x, span_y, depth = potential.shape
    width = HALO_FINE
    packed = exchange(packed_inputs(potential, charge, region, electrode_volts), width)
    potential, charge, region_f, dirichlet = [
        packed[:, :, i * depth:(i + 1) * depth] for i in range(4)
    ]
    movable = jnp.logical_and(region_f == 0.0, inside(span_x, span_y, width))
    flat_sum, vertical = neighbour_sums(pad_plane(potential))
    source = (
        charge - (6.0 * potential - (flat_sum + vertical)) - screen * (jnp.exp(potential) - 1.0)
    )
    coefficient = screen * jnp.exp(potential)
    divisor = 4.0 * 1.0 + 2.0 + coefficient
    iterate = sweeps(dirichlet, source, divisor, 1.0, movable, 1)
    near = [interior(values, width - 2) for values in (iterate, source, divisor, movable)]
    residual = residual_of(near[0], near[1], near[2], 1.0, near[3])
    source_1 = restrict(residual, 2, 2, span_x, span_y)
    coefficient_1 = coarsen(interior(coefficient, width))

    level_1 = descend(1, source_1, coefficient_1, HALO_MID)
    source_2, coefficient_2 = level_1[5], level_1[6]
    span_x2 = source_2.shape[0]
    whole = gather_x(jnp.concatenate([source_2, coefficient_2], axis=2))
    level_2 = descend_whole_x(2, whole[:, :, :depth], whole[:, :, depth:], HALO_MID)
    iterate_3 = coarsest_whole_x(level_2[5], level_2[6], HALO_COARSE)

    rim = HALO_MID // 2
    iterate_2, source_2, divisor_2, allowed_2 = [
        values[:, rim:values.shape[1] - rim] for values in (level_2[0], level_2[1], level_2[2], level_2[4])
    ]
    weight_2 = level_2[3]
    iterate_3 = iterate_3[:, 1:iterate_3.shape[1] - 1]
    iterate_2 = sweeps(iterate_2 + lift(iterate_3), source_2, divisor_2, weight_2, allowed_2, 1)
    iterate_2 = exchange_y(iterate_2[:, rim:source_2.shape[1] - rim], rim)
    iterate_2 = x_window(iterate_2, lax.axis_index("gx") * span_x2, span_x2 + 2 * rim, rim)

    iterate_1, source_1, divisor_1, weight_1, allowed_1 = level_1[:5]
    iterate_1 = sweeps(iterate_1 + lift(iterate_2), source_1, divisor_1, weight_1, allowed_1, 1)
    cut = width - 2
    lifted = lift(interior(iterate_1, HALO_MID - 1))
    movable = interior(movable, cut)
    iterate = interior(iterate, cut) + jnp.where(movable, lifted, 0.0)
    iterate = sweeps(iterate, interior(source, cut), interior(divisor, cut), 1.0, movable, 1)
    return interior(iterate, 2)


def solution(mesh):
    placed = (P("gx", "gy", None), P("gx", "gy", None), P("gx", "gy", None), P())
    return jax.shard_map(
        body, mesh=mesh, in_specs=placed, out_specs=P("gx", "gy", None), check_vma=False
    )
```

```python
import jax
import jax.numpy as jnp
from jax import lax
from jax.experimental import pallas as pl
from jax.experimental.pallas import tpu as pltpu
from jax.sharding import PartitionSpec as P

screen = 0.5

HALO_FINE = 4
HALO_MID = 4
HALO_COARSE = 4


def shifted(block, axis, distance):
    count = lax.axis_size(axis)
    route = [(i, i + distance) for i in range(count) if 0 <= i + distance < count]
    if not route:
        return jnp.zeros_like(block)
    return lax.ppermute(block, axis, route)


def exchange(block, width):
    block = jnp.concatenate(
        [shifted(block[:, -width:], "gy", 1), block, shifted(block[:, :width], "gy", -1)], axis=1
    )
    return jnp.concatenate(
        [shifted(block[-width:], "gx", 1), block, shifted(block[:width], "gx", -1)], axis=0
    )


def along(block, width, axis, dim):
    span = block.shape[dim]
    reach = -(-width // span)
    part = width - (reach - 1) * span
    low = [shifted(lax.slice_in_dim(block, span - part, span, axis=dim), axis, reach)]
    low += [shifted(block, axis, d) for d in range(reach - 1, 0, -1)]
    high = [shifted(block, axis, -d) for d in range(1, reach)]
    high += [shifted(lax.slice_in_dim(block, 0, part, axis=dim), axis, -reach)]
    return jnp.concatenate(low + [block] + high, axis=dim)


def exchange_y(block, width):
    return jnp.concatenate(
        [shifted(block[:, -width:], "gy", 1), block, shifted(block[:, :width], "gy", -1)], axis=1
    )


def gather_x(block):
    count, index = lax.axis_size("gx"), lax.axis_index("gx")
    group = 1
    while group < count:
        size = min(4, count // group)
        received = [block] + [
            lax.ppermute(block, "gx", [(i, i ^ (m * group)) for i in range(count)])
            for m in range(1, size)
        ]
        stacked = jnp.stack(received)
        own = (index // group) % size
        block = jnp.concatenate(
            [lax.dynamic_index_in_dim(stacked, q ^ own, keepdims=False) for q in range(size)], axis=0
        )
        group *= size
    return block


def exchange_many(arrays, width, exchanger=exchange):
    depth = arrays[0].shape[2]
    packed = exchanger(jnp.concatenate(arrays, axis=2), width)
    return [packed[:, :, i * depth:(i + 1) * depth] for i in range(len(arrays))]


def inside(span_x, span_y, width, whole_x=False):
    index_y = lax.axis_index("gy") * span_y - width + jnp.arange(span_y + 2 * width)
    total_y = span_y * lax.axis_size("gy")
    keep_y = (index_y >= 0) & (index_y < total_y)
    if whole_x:
        return jnp.broadcast_to(keep_y[None, :, None], (span_x, span_y + 2 * width, 1))
    index_x = lax.axis_index("gx") * span_x - width + jnp.arange(span_x + 2 * width)
    total_x = span_x * lax.axis_size("gx")
    keep_x = (index_x >= 0) & (index_x < total_x)
    return (keep_x[:, None] & keep_y[None, :])[:, :, None]


def pad_plane(values):
    return jnp.pad(values, ((1, 1), (1, 1), (0, 0)))


def neighbour_sums(padded):
    interior = padded[1:-1, 1:-1]
    flat_sum = padded[2:, 1:-1] + padded[:-2, 1:-1] + padded[1:-1, 2:] + padded[1:-1, :-2]
    padded_z = jnp.pad(interior, ((0, 0), (0, 0), (1, 1)))
    vertical = padded_z[:, :, 2:] + padded_z[:, :, :-2]
    return (flat_sum, vertical)


def checker(span_x, span_y, span_z):
    index_x = jnp.arange(span_x, dtype=jnp.int32)[:, None, None]
    index_y = jnp.arange(span_y, dtype=jnp.int32)[None, :, None]
    index_z = jnp.arange(span_z, dtype=jnp.int32)[None, None, :]
    return (index_x + index_y + index_z) % 2


def half_sweep(iterate, source, divisor, weight, allowed, colour):
    flat_sum, vertical = neighbour_sums(pad_plane(iterate))
    renewed = (source + weight * flat_sum + vertical) / divisor
    span_x, span_y, span_z = iterate.shape
    update = jnp.logical_and(checker(span_x, span_y, span_z) == colour, allowed)
    return jnp.where(update, renewed, iterate)


def sweeps(iterate, source, divisor, weight, allowed, count):
    for _ in range(count):
        iterate = half_sweep(iterate, source, divisor, weight, allowed, 0)
        iterate = half_sweep(iterate, source, divisor, weight, allowed, 1)
    return iterate


def residual_of(iterate, source, divisor, weight, allowed):
    flat_sum, vertical = neighbour_sums(pad_plane(iterate))
    residual = source - (divisor * iterate - (weight * flat_sum + vertical))
    return jnp.where(allowed, residual, 0.0)


def restrict(values, width_x, width_y, span_x, span_y):
    rows = values[width_x - 1:width_x + span_x, width_y - 1:width_y + span_y]
    cols = 0.25 * rows[0:-1:2] + 0.5 * rows[1::2] + 0.25 * rows[2::2]
    return 0.25 * cols[:, 0:-1:2] + 0.5 * cols[:, 1::2] + 0.25 * cols[:, 2::2]


def coarsen(values):
    across = 0.5 * (values[0::2] + values[1::2])
    return 0.5 * (across[:, 0::2] + across[:, 1::2])


def lift(coarse):
    return jnp.repeat(jnp.repeat(coarse, 2, axis=0), 2, axis=1)


def interior(values, width):
    return values[width:values.shape[0] - width, width:values.shape[1] - width]


def descend(grid_level, source, coefficient, width):
    span_x, span_y = source.shape[0], source.shape[1]
    source, coefficient_ext = exchange_many([source, coefficient], width)
    weight = 0.25**grid_level
    divisor = 4.0 * weight + 2.0 + coefficient_ext
    allowed = inside(span_x, span_y, width)
    iterate = sweeps(jnp.zeros_like(source), source, divisor, weight, allowed, 1)
    residual = residual_of(iterate, source, divisor, weight, allowed)
    coarse_source = restrict(residual, width, width, span_x, span_y)
    coarse_coefficient = coarsen(interior(coefficient_ext, width))
    return iterate, source, divisor, weight, allowed, coarse_source, coarse_coefficient


def descend_whole_x(grid_level, source, coefficient, width):
    span_y = source.shape[1]
    source, coefficient = exchange_many([source, coefficient], width, exchange_y)
    span_x = source.shape[0]
    weight = 0.25**grid_level
    divisor = 4.0 * weight + 2.0 + coefficient
    allowed = inside(span_x, span_y, width, whole_x=True)
    iterate = sweeps(jnp.zeros_like(source), source, divisor, weight, allowed, 1)
    residual = residual_of(iterate, source, divisor, weight, allowed)
    residual = jnp.pad(residual, ((1, 0), (0, 0), (0, 0)))
    coarse_source = restrict(residual, 1, width, span_x, span_y)
    coarse_coefficient = coarsen(coefficient[:, width:width + span_y])
    return iterate, source, divisor, weight, allowed, coarse_source, coarse_coefficient


def coarsest_whole_x(source, coefficient, width):
    span_y = source.shape[1]
    exchanger = lambda block, rim: along(block, rim, "gy", 1)
    source, coefficient = exchange_many([source, coefficient], width, exchanger)
    span_x = source.shape[0]
    weight = 0.25**3
    divisor = 4.0 * weight + 2.0 + coefficient
    allowed = inside(span_x, span_y, width, whole_x=True)
    iterate = jnp.zeros_like(source)
    plan = [(0, 1, 0, 1, 0), (1, 0, 1)]
    for step, colours in enumerate(plan):
        if step > 0:
            iterate = exchanger(iterate[:, width:width + span_y], width)
        for colour in colours:
            iterate = half_sweep(iterate, source, divisor, weight, allowed, colour)
    cut = width - 2
    return iterate[:, cut:iterate.shape[1] - cut]


def x_window(values, start, length, margin):
    padded = jnp.pad(values, ((margin, margin), (0, 0), (0, 0)))
    return lax.dynamic_slice_in_dim(padded, start, length, axis=0)


def dirichlet_kernel(volts_ref, potential_ref, charge_ref, region_ref, packed_ref):
    region = region_ref[...]
    total = jnp.zeros(region.shape, jnp.float32)
    for electrode in range(volts_ref.shape[0]):
        total = total + jnp.where(region == electrode + 1, volts_ref[electrode], jnp.float32(0.0))
    depth = region.shape[2]
    packed_ref[:, :, 0:depth] = potential_ref[...]
    packed_ref[:, :, depth:2 * depth] = charge_ref[...]
    packed_ref[:, :, 2 * depth:3 * depth] = region.astype(jnp.float32)
    packed_ref[:, :, 3 * depth:4 * depth] = total


def packed_inputs(potential, charge, region, electrode_volts):
    span_x, span_y, depth = potential.shape
    vmem = pl.BlockSpec(memory_space=pltpu.VMEM)
    return pl.pallas_call(
        dirichlet_kernel,
        out_shape=jax.ShapeDtypeStruct((span_x, span_y, 4 * depth), jnp.float32),
        in_specs=[pl.BlockSpec(memory_space=pltpu.SMEM), vmem, vmem, vmem],
        out_specs=vmem,
    )(electrode_volts, potential, charge, region)


def body(potential, charge, region, electrode_volts):
    span_x, span_y, depth = potential.shape
    width = HALO_FINE
    packed = exchange(packed_inputs(potential, charge, region, electrode_volts), width)
    potential, charge, region_f, dirichlet = [
        packed[:, :, i * depth:(i + 1) * depth] for i in range(4)
    ]
    movable = jnp.logical_and(region_f == 0.0, inside(span_x, span_y, width))
    flat_sum, vertical = neighbour_sums(pad_plane(potential))
    source = (
        charge - (6.0 * potential - (flat_sum + vertical)) - screen * (jnp.exp(potential) - 1.0)
    )
    coefficient = screen * jnp.exp(potential)
    divisor = 4.0 * 1.0 + 2.0 + coefficient
    iterate = sweeps(dirichlet, source, divisor, 1.0, movable, 1)
    residual = residual_of(iterate, source, divisor, 1.0, movable)
    source_1 = restrict(residual, width, width, span_x, span_y)
    coefficient_1 = coarsen(interior(coefficient, width))

    level_1 = descend(1, source_1, coefficient_1, HALO_MID)
    source_2, coefficient_2 = level_1[5], level_1[6]
    span_x2 = source_2.shape[0]
    whole = gather_x(jnp.concatenate([source_2, coefficient_2], axis=2))
    level_2 = descend_whole_x(2, whole[:, :, :depth], whole[:, :, depth:], HALO_MID)
    iterate_3 = coarsest_whole_x(level_2[5], level_2[6], HALO_COARSE)

    iterate_2, source_2, divisor_2, weight_2, allowed_2 = level_2[:5]
    iterate_2 = sweeps(iterate_2 + lift(iterate_3), source_2, divisor_2, weight_2, allowed_2, 1)
    rim = HALO_MID // 2
    iterate_2 = exchange_y(iterate_2[:, HALO_MID:HALO_MID + source_2.shape[1] - 2 * HALO_MID], rim)
    iterate_2 = x_window(iterate_2, lax.axis_index("gx") * span_x2, span_x2 + 2 * rim, rim)

    iterate_1, source_1, divisor_1, weight_1, allowed_1 = level_1[:5]
    iterate_1 = sweeps(iterate_1 + lift(iterate_2), source_1, divisor_1, weight_1, allowed_1, 1)
    cut = width - 2
    lifted = lift(interior(iterate_1, HALO_MID - 1))
    movable = interior(movable, cut)
    iterate = interior(iterate, cut) + jnp.where(movable, lifted, 0.0)
    iterate = sweeps(iterate, interior(source, cut), interior(divisor, cut), 1.0, movable, 1)
    return interior(iterate, 2)


def solution(mesh):
    placed = (P("gx", "gy", None), P("gx", "gy", None), P("gx", "gy", None), P())
    return jax.shard_map(
        body, mesh=mesh, in_specs=placed, out_specs=P("gx", "gy", None), check_vma=False
    )
```

```python
import jax
import jax.numpy as jnp
from jax import lax
from jax.experimental import pallas as pl
from jax.experimental.pallas import tpu as pltpu
from jax.sharding import PartitionSpec as P

screen = 0.5

HALO_FINE = 4
HALO_MID = 4
HALO_COARSE = 4


def shifted(block, axis, distance):
    count = lax.axis_size(axis)
    route = [(i, i + distance) for i in range(count) if 0 <= i + distance < count]
    if not route:
        return jnp.zeros_like(block)
    return lax.ppermute(block, axis, route)


def exchange(block, width):
    block = jnp.concatenate(
        [shifted(block[-width:], "gx", 1), block, shifted(block[:width], "gx", -1)], axis=0
    )
    return jnp.concatenate(
        [shifted(block[:, -width:], "gy", 1), block, shifted(block[:, :width], "gy", -1)], axis=1
    )


def along(block, width, axis, dim):
    span = block.shape[dim]
    reach = -(-width // span)
    part = width - (reach - 1) * span
    low = [shifted(lax.slice_in_dim(block, span - part, span, axis=dim), axis, reach)]
    low += [shifted(block, axis, d) for d in range(reach - 1, 0, -1)]
    high = [shifted(block, axis, -d) for d in range(1, reach)]
    high += [shifted(lax.slice_in_dim(block, 0, part, axis=dim), axis, -reach)]
    return jnp.concatenate(low + [block] + high, axis=dim)


def exchange_y(block, width):
    return jnp.concatenate(
        [shifted(block[:, -width:], "gy", 1), block, shifted(block[:, :width], "gy", -1)], axis=1
    )


def gather_x(block):
    count, index = lax.axis_size("gx"), lax.axis_index("gx")
    group = 1
    while group < count:
        size = min(4, count // group)
        received = [block] + [
            lax.ppermute(block, "gx", [(i, i ^ (m * group)) for i in range(count)])
            for m in range(1, size)
        ]
        stacked = jnp.stack(received)
        own = (index // group) % size
        block = jnp.concatenate(
            [lax.dynamic_index_in_dim(stacked, q ^ own, keepdims=False) for q in range(size)], axis=0
        )
        group *= size
    return block


def exchange_many(arrays, width, exchanger=exchange):
    depth = arrays[0].shape[2]
    packed = exchanger(jnp.concatenate(arrays, axis=2), width)
    return [packed[:, :, i * depth:(i + 1) * depth] for i in range(len(arrays))]


def inside(span_x, span_y, width, whole_x=False):
    index_y = lax.axis_index("gy") * span_y - width + jnp.arange(span_y + 2 * width)
    total_y = span_y * lax.axis_size("gy")
    keep_y = (index_y >= 0) & (index_y < total_y)
    if whole_x:
        return jnp.broadcast_to(keep_y[None, :, None], (span_x, span_y + 2 * width, 1))
    index_x = lax.axis_index("gx") * span_x - width + jnp.arange(span_x + 2 * width)
    total_x = span_x * lax.axis_size("gx")
    keep_x = (index_x >= 0) & (index_x < total_x)
    return (keep_x[:, None] & keep_y[None, :])[:, :, None]


def pad_plane(values):
    return jnp.pad(values, ((1, 1), (1, 1), (0, 0)))


def neighbour_sums(padded):
    interior = padded[1:-1, 1:-1]
    flat_sum = padded[2:, 1:-1] + padded[:-2, 1:-1] + padded[1:-1, 2:] + padded[1:-1, :-2]
    padded_z = jnp.pad(interior, ((0, 0), (0, 0), (1, 1)))
    vertical = padded_z[:, :, 2:] + padded_z[:, :, :-2]
    return (flat_sum, vertical)


def checker(span_x, span_y, span_z):
    index_x = jnp.arange(span_x, dtype=jnp.int32)[:, None, None]
    index_y = jnp.arange(span_y, dtype=jnp.int32)[None, :, None]
    index_z = jnp.arange(span_z, dtype=jnp.int32)[None, None, :]
    return (index_x + index_y + index_z) % 2


def half_sweep(iterate, source, divisor, weight, allowed, colour):
    flat_sum, vertical = neighbour_sums(pad_plane(iterate))
    renewed = (source + weight * flat_sum + vertical) / divisor
    span_x, span_y, span_z = iterate.shape
    update = jnp.logical_and(checker(span_x, span_y, span_z) == colour, allowed)
    return jnp.where(update, renewed, iterate)


def sweeps(iterate, source, divisor, weight, allowed, count):
    for _ in range(count):
        iterate = half_sweep(iterate, source, divisor, weight, allowed, 0)
        iterate = half_sweep(iterate, source, divisor, weight, allowed, 1)
    return iterate


def residual_of(iterate, source, divisor, weight, allowed):
    flat_sum, vertical = neighbour_sums(pad_plane(iterate))
    residual = source - (divisor * iterate - (weight * flat_sum + vertical))
    return jnp.where(allowed, residual, 0.0)


def restrict(values, width_x, width_y, span_x, span_y):
    rows = values[width_x - 1:width_x + span_x, width_y - 1:width_y + span_y]
    cols = 0.25 * rows[0:-1:2] + 0.5 * rows[1::2] + 0.25 * rows[2::2]
    return 0.25 * cols[:, 0:-1:2] + 0.5 * cols[:, 1::2] + 0.25 * cols[:, 2::2]


def coarsen(values):
    across = 0.5 * (values[0::2] + values[1::2])
    return 0.5 * (across[:, 0::2] + across[:, 1::2])


def lift(coarse):
    return jnp.repeat(jnp.repeat(coarse, 2, axis=0), 2, axis=1)


def interior(values, width):
    return values[width:values.shape[0] - width, width:values.shape[1] - width]


def descend(grid_level, source, coefficient, width):
    span_x, span_y = source.shape[0], source.shape[1]
    source, coefficient_ext = exchange_many([source, coefficient], width)
    weight = 0.25**grid_level
    divisor = 4.0 * weight + 2.0 + coefficient_ext
    allowed = inside(span_x, span_y, width)
    iterate = sweeps(jnp.zeros_like(source), source, divisor, weight, allowed, 1)
    residual = residual_of(iterate, source, divisor, weight, allowed)
    coarse_source = restrict(residual, width, width, span_x, span_y)
    coarse_coefficient = coarsen(interior(coefficient_ext, width))
    return iterate, source, divisor, weight, allowed, coarse_source, coarse_coefficient


def descend_whole_x(grid_level, source, coefficient, width):
    span_y = source.shape[1]
    source, coefficient = exchange_many([source, coefficient], width, exchange_y)
    span_x = source.shape[0]
    weight = 0.25**grid_level
    divisor = 4.0 * weight + 2.0 + coefficient
    allowed = inside(span_x, span_y, width, whole_x=True)
    iterate = sweeps(jnp.zeros_like(source), source, divisor, weight, allowed, 1)
    residual = residual_of(iterate, source, divisor, weight, allowed)
    residual = jnp.pad(residual, ((1, 0), (0, 0), (0, 0)))
    coarse_source = restrict(residual, 1, width, span_x, span_y)
    coarse_coefficient = coarsen(coefficient[:, width:width + span_y])
    return iterate, source, divisor, weight, allowed, coarse_source, coarse_coefficient


def coarsest_whole_x(source, coefficient, width):
    span_y = source.shape[1]
    exchanger = lambda block, rim: along(block, rim, "gy", 1)
    source, coefficient = exchange_many([source, coefficient], width, exchanger)
    span_x = source.shape[0]
    weight = 0.25**3
    divisor = 4.0 * weight + 2.0 + coefficient
    allowed = inside(span_x, span_y, width, whole_x=True)
    iterate = jnp.zeros_like(source)
    plan = [(0, 1, 0, 1, 0), (1, 0, 1)]
    for step, colours in enumerate(plan):
        if step > 0:
            iterate = exchanger(iterate[:, width:width + span_y], width)
        for colour in colours:
            iterate = half_sweep(iterate, source, divisor, weight, allowed, colour)
    cut = width - 2
    return iterate[:, cut:iterate.shape[1] - cut]


def x_window(values, start, length, margin):
    padded = jnp.pad(values, ((margin, margin), (0, 0), (0, 0)))
    return lax.dynamic_slice_in_dim(padded, start, length, axis=0)


def dirichlet_kernel(volts_ref, potential_ref, charge_ref, region_ref, packed_ref):
    region = region_ref[...]
    total = jnp.zeros(region.shape, jnp.float32)
    for electrode in range(volts_ref.shape[0]):
        total = total + jnp.where(region == electrode + 1, volts_ref[electrode], jnp.float32(0.0))
    depth = region.shape[2]
    packed_ref[:, :, 0:depth] = potential_ref[...]
    packed_ref[:, :, depth:2 * depth] = charge_ref[...]
    packed_ref[:, :, 2 * depth:3 * depth] = region.astype(jnp.float32)
    packed_ref[:, :, 3 * depth:4 * depth] = total


def packed_inputs(potential, charge, region, electrode_volts):
    span_x, span_y, depth = potential.shape
    vmem = pl.BlockSpec(memory_space=pltpu.VMEM)
    return pl.pallas_call(
        dirichlet_kernel,
        out_shape=jax.ShapeDtypeStruct((span_x, span_y, 4 * depth), jnp.float32),
        in_specs=[pl.BlockSpec(memory_space=pltpu.SMEM), vmem, vmem, vmem],
        out_specs=vmem,
    )(electrode_volts, potential, charge, region)


def body(potential, charge, region, electrode_volts):
    span_x, span_y, depth = potential.shape
    width = HALO_FINE
    packed = exchange(packed_inputs(potential, charge, region, electrode_volts), width)
    potential, charge, region_f, dirichlet = [
        packed[:, :, i * depth:(i + 1) * depth] for i in range(4)
    ]
    movable = jnp.logical_and(region_f == 0.0, inside(span_x, span_y, width))
    flat_sum, vertical = neighbour_sums(pad_plane(potential))
    source = (
        charge - (6.0 * potential - (flat_sum + vertical)) - screen * (jnp.exp(potential) - 1.0)
    )
    coefficient = screen * jnp.exp(potential)
    divisor = 4.0 * 1.0 + 2.0 + coefficient
    iterate = sweeps(dirichlet, source, divisor, 1.0, movable, 1)
    near = [interior(values, width - 2) for values in (iterate, source, divisor, movable)]
    residual = residual_of(near[0], near[1], near[2], 1.0, near[3])
    source_1 = restrict(residual, 2, 2, span_x, span_y)
    coefficient_1 = coarsen(interior(coefficient, width))

    level_1 = descend(1, source_1, coefficient_1, HALO_MID)
    source_2, coefficient_2 = level_1[5], level_1[6]
    span_x2 = source_2.shape[0]
    whole = gather_x(jnp.concatenate([source_2, coefficient_2], axis=2))
    level_2 = descend_whole_x(2, whole[:, :, :depth], whole[:, :, depth:], HALO_MID)
    iterate_3 = coarsest_whole_x(level_2[5], level_2[6], HALO_COARSE)

    iterate_2, source_2, divisor_2, weight_2, allowed_2 = level_2[:5]
    iterate_2 = sweeps(iterate_2 + lift(iterate_3), source_2, divisor_2, weight_2, allowed_2, 1)
    rim = HALO_MID // 2
    iterate_2 = exchange_y(iterate_2[:, HALO_MID:HALO_MID + source_2.shape[1] - 2 * HALO_MID], rim)
    iterate_2 = x_window(iterate_2, lax.axis_index("gx") * span_x2, span_x2 + 2 * rim, rim)

    iterate_1, source_1, divisor_1, weight_1, allowed_1 = level_1[:5]
    iterate_1 = sweeps(iterate_1 + lift(iterate_2), source_1, divisor_1, weight_1, allowed_1, 1)
    cut = width - 2
    lifted = lift(interior(iterate_1, HALO_MID - 1))
    movable = interior(movable, cut)
    iterate = interior(iterate, cut) + jnp.where(movable, lifted, 0.0)
    iterate = sweeps(iterate, interior(source, cut), interior(divisor, cut), 1.0, movable, 1)
    return interior(iterate, 2)


def solution(mesh):
    placed = (P("gx", "gy", None), P("gx", "gy", None), P("gx", "gy", None), P())
    return jax.shard_map(
        body, mesh=mesh, in_specs=placed, out_specs=P("gx", "gy", None), check_vma=False
    )
```
